512 devices in a mesh: src: 32 (over y, x_lo, core), rcv: 8 (over z), int: 2 (over x_hi).
Axes of the slice: x: 4 (x_hi: 2, x_lo: 2; x = x_hi * 2 + x_lo), y: 8, z: 8, core: 2. Of those that a mesh axis runs over, the one named last changes fastest.
Arguments:
- traces: float32 [2, 1, 4096, 4096], P(None, None, 'src', 'rcv'), may hold values from -6 to 6
- missing: int32 [32, 32], P('src', 'rcv'), may hold values from 0 to 1, as said below
- aperture: int32 [32, 24], P('src'), may hold values from 0 to 32, as said below
- wavelet: float32 [2, 1], replicated, may hold values from -0.06 to 0.06
Outputs:
- primaries: float32 [2, 1, 4096, 4096], P(None, None, 'src', ('rcv', 'int'))
The draws below stay inside these ranges and needn't reach their ends.
Inputs may be any that keep to these rules, and one draw needn't show every extreme that they name: `missing`: A tile is marked only where its receiver block lies above its source block, so the mirrored tile is always recorded; some tile is marked. `aperture`: in each row the listed blocks come first and are distinct; the remaining entries are the padding value 32. Each row lists 24 // 2 to 24 blocks; some row lists exactly 24 and some row exactly 12.
All inputs are finite; a program needn't handle non-finite values.
Results may differ from the reference program's by a relative error of at most 0.00005.
Values sent between devices are 32-bit elements; how exact they have to be, the bound alone decides.
No kernel may reach another device: no remote copies, remote signals or barrier semaphores. Data moves between devices by JAX's collectives and lax.ppermute only.
A program may use at most 64 MiB of HBM per device.

```python
import jax
import jax.numpy as jnp
from jax import lax

GRID = 4096
TILE = 128
APER = 24
NFREQ = 1


def draw_missing(key, part):
    block_count = GRID // TILE
    coins = jax.random.randint(jax.random.fold_in(key, 11), (block_count, block_count), 0, 3)
    upper = jnp.arange(block_count)[None, :] > jnp.arange(block_count)[:, None]
    marks = jnp.where((coins == 0) & upper, 1, 0).astype(jnp.int32)
    return marks.at[0, block_count - 1].set(1)


def draw_aperture(key, part):
    block_count = GRID // TILE
    row_keys = jax.random.split(jax.random.fold_in(key, 23), block_count)
    orders = jax.vmap(lambda one_key: jax.random.permutation(one_key, block_count))(row_keys).astype(jnp.int32)
    counts = jax.random.randint(jax.random.fold_in(key, 37), (block_count,), APER // 2, APER + 1)
    counts = counts.at[0].set(APER).at[block_count - 1].set(APER // 2)
    slots = jnp.arange(APER)[None, :]
    return jnp.where(slots < counts[:, None], orders[:, :APER], block_count).astype(jnp.int32)


def block_scale(own_key, shape, pieces, least, high):
    level, own = 1.0, jax.random.fold_in(own_key, 6)
    for position, blocks in pieces:
        draws = jnp.exp(jax.random.uniform(jax.random.fold_in(own, position), (blocks,), jnp.float32, least / len(pieces), high / len(pieces)))
        level = level * jnp.repeat(draws, shape[position] // blocks).reshape([-1 if axis == position else 1 for axis in range(len(shape))])
    return level


def centred(own_key, extent, scale, most, pieces=(), kind=jnp.bfloat16):
    gain = block_scale(own_key, extent, pieces, -0.22, 0.18) if pieces else 1.0
    entries = jax.random.normal(own_key, extent, jnp.float32) * scale * gain
    return jnp.minimum(jnp.maximum(entries, -most), most).astype(kind)


def setup_inputs(seed: int = 0) -> dict:
    keys = jax.random.split(jax.random.key(seed), 5)
    traces = centred(keys[0], (2, NFREQ, GRID, GRID), 1.0, 6.0, ((2, 32), (3, 8)), jnp.float32)
    missing = draw_missing(jax.random.fold_in(keys[4], 71), 0)
    aperture = draw_aperture(jax.random.fold_in(keys[4], 71), 0)
    wavelet = centred(keys[3], (2, NFREQ), 0.0125, 0.06, (), jnp.float32)
    return dict(traces=traces, missing=missing, aperture=aperture, wavelet=wavelet)


def complex_prod(left_side, right_side):
    return jnp.einsum("fik,fkj->fij", left_side, right_side, precision=lax.Precision.HIGHEST)


def reference(traces, missing, aperture, wavelet):
    block_count = GRID // TILE
    mirrored = jnp.swapaxes(traces, 2, 3)
    tile_mask = jnp.repeat(jnp.repeat(missing, TILE, axis=0), TILE, axis=1) > 0
    filled = jnp.where(tile_mask[None, None], mirrored, traces)
    chosen = (aperture[:, :, None] == jnp.arange(block_count, dtype=jnp.int32)[None, None, :]).astype(jnp.float32).sum(axis=1)
    chosen_full = jnp.repeat(jnp.repeat(chosen, TILE, axis=0), TILE, axis=1)
    weighted = filled * chosen_full[None, None]
    pred_real = complex_prod(weighted[0], filled[0]) - complex_prod(weighted[1], filled[1])
    pred_imag = complex_prod(weighted[0], filled[1]) + complex_prod(weighted[1], filled[0])
    w_real = wavelet[0][:, None, None]
    w_imag = wavelet[1][:, None, None]
    out_real = filled[0] - (w_real * pred_real - w_imag * pred_imag)
    out_imag = filled[1] - (w_real * pred_imag + w_imag * pred_real)
    return jnp.stack([out_real, out_imag])
```

```python
import jax
import jax.numpy as jnp
import numpy as np
from jax import lax
from jax.sharding import Mesh
from jax.sharding import PartitionSpec as P

TILE = 128
SRC = ("y", "xl", "c")
FILL = ("y", "xl", "c", "z")


def mirror_pairs(n_src, n_rcv, per_rcv, step):
    pairs = []
    for s in range(n_src):
        for r in range(n_rcv):
            t = (s % per_rcv + step) % per_rcv
            dest_s = per_rcv * r + t
            if s > dest_s:
                pairs.append((s * n_rcv + r, dest_s * n_rcv + s // per_rcv))
    return pairs


def per_device(traces, missing, aperture, wavelet):
    n_src = lax.axis_size(SRC)
    n_rcv = lax.axis_size("z")
    n_half = lax.axis_size("xh")
    n_core = lax.axis_size("c")
    me_src = lax.axis_index(SRC)
    me_rcv = lax.axis_index("z")
    my_half = lax.axis_index("xh")
    comp_count, freq_count, local_rows, local_cols = traces.shape
    assert local_rows == TILE
    per_rcv = local_cols // TILE
    tiles = traces.reshape(comp_count, freq_count, TILE, per_rcv, TILE)

    arrived = []
    for step in range(per_rcv):
        pick = (me_src % per_rcv + step) % per_rcv
        sent = lax.dynamic_index_in_dim(tiles, pick, 3, keepdims=False)
        got = lax.ppermute(sent, FILL, mirror_pairs(n_src, n_rcv, per_rcv, step))
        arrived.append(jnp.swapaxes(got, 2, 3))
    arrived = jnp.stack(arrived, axis=3)
    order = (me_src % per_rcv - jnp.arange(per_rcv)) % per_rcv
    mirrored = jnp.take(arrived, order, axis=3)
    marks = (missing[0] > 0)[None, None, None, :, None]
    filled = jnp.where(marks, mirrored, tiles)

    first = me_rcv * per_rcv
    local_blocks = first + jnp.arange(per_rcv, dtype=jnp.int32)
    chosen = (aperture[0][:, None] == local_blocks[None, :]).astype(jnp.float32).sum(axis=0)

    half = TILE // n_half
    left = filled.reshape(comp_count, freq_count, TILE, per_rcv, n_half, half)
    left = lax.dynamic_index_in_dim(left, my_half, 4, keepdims=False)
    left = left * chosen[None, None, None, :, None]
    left = left.reshape(comp_count, freq_count, TILE, per_rcv * half)
    left = lax.all_gather(left, "z", axis=3, tiled=True)
    n_pair = n_src // n_core
    left = left.reshape(comp_count, freq_count, TILE, n_pair, n_core, half)
    left = jnp.transpose(left, (1, 0, 2, 4, 3, 5))
    left = left.reshape(freq_count, comp_count * TILE, n_src * half)

    right = filled.reshape(comp_count, freq_count, n_half, half, local_cols)
    right = lax.dynamic_index_in_dim(right, my_half, 2, keepdims=False)
    right = jnp.transpose(right, (1, 2, 0, 3))
    right = lax.all_gather(right, ("y", "xl"), axis=1, tiled=True)
    right = lax.all_gather(right, "c", axis=1, tiled=False)
    right = right.reshape(freq_count, n_src * half, comp_count * local_cols)

    prod = jnp.einsum("fak,fkb->fab", left, right, precision=lax.Precision.HIGHEST)
    prod = prod.reshape(freq_count, comp_count, TILE, comp_count, local_cols)
    real_part = prod[:, 0, :, 0] - prod[:, 1, :, 1]
    imag_part = prod[:, 0, :, 1] + prod[:, 1, :, 0]
    partial_sum = jnp.stack([real_part, imag_part])
    my_share = lax.psum_scatter(partial_sum, "xh", scatter_dimension=3, tiled=True)

    out_cols = local_cols // n_half
    kept = filled.reshape(comp_count, freq_count, TILE, local_cols)
    kept = lax.dynamic_slice_in_dim(kept, my_half * out_cols, out_cols, axis=3)
    w_real = wavelet[0][:, None, None]
    w_imag = wavelet[1][:, None, None]
    out_real = kept[0] - (w_real * my_share[0] - w_imag * my_share[1])
    out_imag = kept[1] - (w_real * my_share[1] + w_imag * my_share[0])
    return jnp.stack([out_real, out_imag])


def solution(mesh):
    n_src, n_rcv, n_int = (mesh.shape[a] for a in ("src", "rcv", "int"))
    fine = Mesh(
        np.asarray(mesh.devices).reshape(n_src // 4, 2, 2, n_rcv, n_int),
        ("y", "xl", "c", "z", "xh"),
    )
    placed = (P(None, None, SRC, "z"), P(SRC, "z"), P(SRC, None), P())
    return jax.shard_map(
        per_device,
        mesh=fine,
        in_specs=placed,
        out_specs=P(None, None, SRC, ("z", "xh")),
        check_vma=False,
    )
```

```python
import jax
import jax.numpy as jnp
import numpy as np
from jax import lax
from jax.sharding import Mesh
from jax.sharding import PartitionSpec as P

TILE = 128
SRC = ("y", "xl", "c")
FILL = ("y", "xl", "c", "z")


def mirror_pairs(n_src, n_rcv, per_rcv, step):
    pairs = []
    for s in range(n_src):
        for r in range(n_rcv):
            t = (s % per_rcv + step) % per_rcv
            dest_s = per_rcv * r + t
            if s > dest_s:
                pairs.append((s * n_rcv + r, dest_s * n_rcv + s // per_rcv))
    return pairs


def per_device(traces, missing, aperture, wavelet):
    n_src = lax.axis_size(SRC)
    n_rcv = lax.axis_size("z")
    n_half = lax.axis_size("xh")
    n_core = lax.axis_size("c")
    me_src = lax.axis_index(SRC)
    me_rcv = lax.axis_index("z")
    my_half = lax.axis_index("xh")
    comp_count, freq_count, local_rows, local_cols = traces.shape
    assert local_rows == TILE
    per_rcv = local_cols // TILE
    tiles = traces.reshape(comp_count, freq_count, TILE, per_rcv, TILE)

    arrived = []
    for step in range(per_rcv):
        pick = (me_src % per_rcv + step) % per_rcv
        sent = lax.dynamic_index_in_dim(tiles, pick, 3, keepdims=False)
        got = lax.ppermute(sent, FILL, mirror_pairs(n_src, n_rcv, per_rcv, step))
        arrived.append(jnp.swapaxes(got, 2, 3))
    arrived = jnp.stack(arrived, axis=3)
    order = (me_src % per_rcv - jnp.arange(per_rcv)) % per_rcv
    mirrored = jnp.take(arrived, order, axis=3)
    marks = (missing[0] > 0)[None, None, None, :, None]
    filled = jnp.where(marks, mirrored, tiles)

    first = me_rcv * per_rcv
    local_blocks = first + jnp.arange(per_rcv, dtype=jnp.int32)
    chosen = (aperture[0][:, None] == local_blocks[None, :]).astype(jnp.float32).sum(axis=0)

    half = TILE // n_half
    left = filled.reshape(comp_count, freq_count, TILE, per_rcv, n_half, half)
    left = lax.dynamic_index_in_dim(left, my_half, 4, keepdims=False)
    left = left * chosen[None, None, None, :, None]
    left = left.reshape(comp_count, freq_count, TILE, per_rcv * half)
    left = lax.all_gather(left, "z", axis=0, tiled=False)
    n_pair = n_src // n_core
    left = left.reshape(n_rcv, comp_count, freq_count, TILE, per_rcv // n_core, n_core, half)
    left = jnp.transpose(left, (2, 1, 3, 5, 0, 4, 6))
    left = left.reshape(freq_count, comp_count * TILE, n_src * half)

    right = filled.reshape(comp_count, freq_count, n_half, half, local_cols)
    right = lax.dynamic_index_in_dim(right, my_half, 2, keepdims=False)
    right = jnp.transpose(right, (1, 2, 0, 3)).reshape(freq_count, half, comp_count * local_cols)
    right = lax.all_gather(right, ("y", "xl"), axis=1, tiled=True)
    right = lax.all_gather(right, "c", axis=1, tiled=False)
    right = right.reshape(freq_count, n_src * half, comp_count * local_cols)

    prod = jnp.einsum("fak,fkb->fab", left, right, precision=lax.Precision.HIGHEST)
    prod = prod.reshape(freq_count, comp_count, TILE, comp_count, local_cols)
    real_part = prod[:, 0, :, 0] - prod[:, 1, :, 1]
    imag_part = prod[:, 0, :, 1] + prod[:, 1, :, 0]
    partial_sum = jnp.stack([real_part, imag_part])
    my_share = lax.psum_scatter(partial_sum, "xh", scatter_dimension=3, tiled=True)

    out_cols = local_cols // n_half
    kept = filled.reshape(comp_count, freq_count, TILE, local_cols)
    kept = lax.dynamic_slice_in_dim(kept, my_half * out_cols, out_cols, axis=3)
    w_real = wavelet[0][:, None, None]
    w_imag = wavelet[1][:, None, None]
    out_real = kept[0] - (w_real * my_share[0] - w_imag * my_share[1])
    out_imag = kept[1] - (w_real * my_share[1] + w_imag * my_share[0])
    return jnp.stack([out_real, out_imag])


def solution(mesh):
    n_src, n_rcv, n_int = (mesh.shape[a] for a in ("src", "rcv", "int"))
    fine = Mesh(
        np.asarray(mesh.devices).reshape(n_src // 4, 2, 2, n_rcv, n_int),
        ("y", "xl", "c", "z", "xh"),
    )
    placed = (P(None, None, SRC, "z"), P(SRC, "z"), P(SRC, None), P())
    return jax.shard_map(
        per_device,
        mesh=fine,
        in_specs=placed,
        out_specs=P(None, None, SRC, ("z", "xh")),
        check_vma=False,
    )
```

```python
import jax
import jax.numpy as jnp
from jax import lax
from jax.sharding import PartitionSpec as P

TILE = 128


def from_everyone(x, axis):
    copies = jnp.broadcast_to(x, (lax.axis_size(axis), *x.shape))
    return lax.all_to_all(copies, axis, split_axis=0, concat_axis=0, tiled=True)


def joined_along(pieces, dim):
    pieces = jnp.moveaxis(pieces, 0, dim)
    lengths = pieces.shape
    return pieces.reshape(*lengths[:dim], lengths[dim] * lengths[dim + 1], *lengths[dim + 2 :])


def collect(x, axis, dim):
    pieces = from_everyone(x, axis)
    return joined_along(pieces, dim)


def in_blocks(x, dim, count):
    before, after = (x.shape[:dim], x.shape[dim + 1 :])
    return jnp.moveaxis(x.reshape(*before, count, -1, *after), dim, 0)


def sent_and_summed(x, axis, dim):
    pieces = in_blocks(x, dim, lax.axis_size(axis))
    arrived = lax.all_to_all(pieces, axis, split_axis=0, concat_axis=0, tiled=True)
    return arrived.sum(axis=0)


def mirror_pairs(n_src, n_rcv, per_rcv, step):
    pairs = []
    for s in range(n_src):
        for r in range(n_rcv):
            t = (s % per_rcv + step) % per_rcv
            dest_s = per_rcv * r + t
            if s > dest_s:
                pairs.append((s * n_rcv + r, dest_s * n_rcv + s // per_rcv))
    return pairs


def complex_prod(left_side, right_side):
    return jnp.einsum("fik,fkj->fij", left_side, right_side, precision=lax.Precision.HIGHEST)


def per_device(traces, missing, aperture, wavelet):
    half_count = lax.axis_size("int")
    my_half = lax.axis_index("int")
    rcv_count = lax.axis_size("rcv")
    comp_count, freq_count, local_rows, local_cols = traces.shape
    per_rcv = local_cols // TILE
    src_count = lax.axis_size("src")
    me_src = lax.axis_index("src")
    tiles = traces.reshape(comp_count, freq_count, TILE, per_rcv, TILE)
    arrived = []
    for step in range(per_rcv):
        pick = (me_src % per_rcv + step) % per_rcv
        sent = lax.dynamic_index_in_dim(tiles, pick, 3, keepdims=False)
        got = lax.ppermute(sent, ("src", "rcv"), mirror_pairs(src_count, rcv_count, per_rcv, step))
        arrived.append(jnp.swapaxes(got, 2, 3))
    arrived = jnp.stack(arrived, axis=3)
    order = (me_src % per_rcv - jnp.arange(per_rcv)) % per_rcv
    mirrored = jnp.take(arrived, order, axis=3)
    marks = (missing[0] > 0)[None, None, None, :, None]
    filled = jnp.where(marks, mirrored, tiles).reshape(traces.shape)
    row_tiles = local_rows // TILE
    col_tiles = local_cols // TILE
    half_tile = TILE // half_count
    left_half = filled.reshape(comp_count, freq_count, local_rows, col_tiles, half_count, half_tile)
    left_half = lax.dynamic_index_in_dim(left_half, my_half, 4, keepdims=False)
    left_half = left_half.reshape(comp_count, freq_count, local_rows, col_tiles * half_tile)
    right_half = filled.reshape(
        comp_count, freq_count, row_tiles, half_count, half_tile, local_cols
    )
    right_half = lax.dynamic_index_in_dim(right_half, my_half, 3, keepdims=False)
    right_half = right_half.reshape(comp_count, freq_count, row_tiles * half_tile, local_cols)
    gathered = collect(left_half, "rcv", 3)
    block_count = gathered.shape[3] // half_tile
    chosen = (
        (aperture[:, :, None] == jnp.arange(block_count, dtype=jnp.int32)[None, None, :])
        .astype(jnp.float32)
        .sum(axis=1)
    )
    weighted = gathered.reshape(comp_count, freq_count, row_tiles, TILE, block_count, half_tile)
    weighted = (weighted * chosen[None, None, :, None, :, None]).reshape(
        comp_count, freq_count, local_rows, block_count * half_tile
    )
    slab_piece = lax.all_gather(right_half, "src", axis=2, tiled=True)
    real_part = complex_prod(weighted[0], slab_piece[0]) - complex_prod(weighted[1], slab_piece[1])
    imag_part = complex_prod(weighted[0], slab_piece[1]) + complex_prod(weighted[1], slab_piece[0])
    partial_sum = jnp.stack([real_part, imag_part])
    out_cols = local_cols // half_count
    my_share = sent_and_summed(partial_sum, "int", 3)
    kept_data = filled.reshape(comp_count, freq_count, local_rows, half_count, out_cols)
    kept_data = lax.dynamic_index_in_dim(kept_data, my_half, 3, keepdims=False)
    w_real = wavelet[0][:, None, None]
    w_imag = wavelet[1][:, None, None]
    out_real = kept_data[0] - (w_real * my_share[0] - w_imag * my_share[1])
    out_imag = kept_data[1] - (w_real * my_share[1] + w_imag * my_share[0])
    return jnp.stack([out_real, out_imag])


def solution(mesh):
    placed = (P(None, None, "src", "rcv"), P("src", "rcv"), P("src", None), P())
    return jax.shard_map(
        per_device,
        mesh=mesh,
        in_specs=placed,
        out_specs=P(None, None, "src", ("rcv", "int")),
        check_vma=False,
    )
```

```python
import jax
import jax.numpy as jnp
from jax import lax
from jax.sharding import PartitionSpec as P

TILE = 128


def from_everyone(x, axis):
    copies = jnp.broadcast_to(x, (lax.axis_size(axis), *x.shape))
    return lax.all_to_all(copies, axis, split_axis=0, concat_axis=0, tiled=True)


def joined_along(pieces, dim):
    pieces = jnp.moveaxis(pieces, 0, dim)
    lengths = pieces.shape
    return pieces.reshape(*lengths[:dim], lengths[dim] * lengths[dim + 1], *lengths[dim + 2 :])


def collect(x, axis, dim):
    pieces = from_everyone(x, axis)
    return joined_along(pieces, dim)


def in_blocks(x, dim, count):
    before, after = (x.shape[:dim], x.shape[dim + 1 :])
    return jnp.moveaxis(x.reshape(*before, count, -1, *after), dim, 0)


def sent_and_summed(x, axis, dim):
    pieces = in_blocks(x, dim, lax.axis_size(axis))
    arrived = lax.all_to_all(pieces, axis, split_axis=0, concat_axis=0, tiled=True)
    return arrived.sum(axis=0)


def mirror_pairs(n_src, n_rcv, per_rcv, step):
    pairs = []
    for s in range(n_src):
        for r in range(n_rcv):
            t = (s % per_rcv + step) % per_rcv
            dest_s = per_rcv * r + t
            if s > dest_s:
                pairs.append((s * n_rcv + r, dest_s * n_rcv + s // per_rcv))
    return pairs


def complex_prod(left_side, right_side):
    return jnp.einsum("fik,fkj->fij", left_side, right_side, precision=lax.Precision.HIGHEST)


def per_device(traces, missing, aperture, wavelet):
    half_count = lax.axis_size("int")
    my_half = lax.axis_index("int")
    rcv_count = lax.axis_size("rcv")
    comp_count, freq_count, local_rows, local_cols = traces.shape
    per_rcv = local_cols // TILE
    src_count = lax.axis_size("src")
    me_src = lax.axis_index("src")
    tiles = traces.reshape(comp_count, freq_count, TILE, per_rcv, TILE)
    arrived = []
    for step in range(per_rcv):
        pick = (me_src % per_rcv + step) % per_rcv
        sent = lax.dynamic_index_in_dim(tiles, pick, 3, keepdims=False)
        got = lax.ppermute(sent, ("src", "rcv"), mirror_pairs(src_count, rcv_count, per_rcv, step))
        arrived.append(jnp.swapaxes(got, 2, 3))
    arrived = jnp.stack(arrived, axis=3)
    order = (me_src % per_rcv - jnp.arange(per_rcv)) % per_rcv
    mirrored = jnp.take(arrived, order, axis=3)
    marks = (missing[0] > 0)[None, None, None, :, None]
    filled = jnp.where(marks, mirrored, tiles).reshape(traces.shape)
    row_tiles = local_rows // TILE
    col_tiles = local_cols // TILE
    half_tile = TILE // half_count
    left_half = filled.reshape(comp_count, freq_count, local_rows, col_tiles, half_count, half_tile)
    left_half = lax.dynamic_index_in_dim(left_half, my_half, 4, keepdims=False)
    left_half = left_half.reshape(comp_count, freq_count, local_rows, col_tiles * half_tile)
    right_half = filled.reshape(
        comp_count, freq_count, row_tiles, half_count, half_tile, local_cols
    )
    right_half = lax.dynamic_index_in_dim(right_half, my_half, 3, keepdims=False)
    right_half = right_half.reshape(comp_count, freq_count, row_tiles * half_tile, local_cols)
    gathered = collect(left_half, "rcv", 3)
    block_count = gathered.shape[3] // half_tile
    chosen = (
        (aperture[:, :, None] == jnp.arange(block_count, dtype=jnp.int32)[None, None, :])
        .astype(jnp.float32)
        .sum(axis=1)
    )
    weighted = gathered.reshape(comp_count, freq_count, row_tiles, TILE, block_count, half_tile)
    weighted = (weighted * chosen[None, None, :, None, :, None]).reshape(
        comp_count, freq_count, local_rows, block_count * half_tile
    )
    slab_piece = lax.all_gather(right_half, "src", axis=2, tiled=True)
    out_cols = local_cols // half_count
    assert half_count == 2

    def half_product(which):
        cols = slab_piece.reshape(comp_count, freq_count, -1, half_count, out_cols)
        cols = lax.dynamic_index_in_dim(cols, which, 3, keepdims=False)
        real_part = complex_prod(weighted[0], cols[0]) - complex_prod(weighted[1], cols[1])
        imag_part = complex_prod(weighted[0], cols[1]) + complex_prod(weighted[1], cols[0])
        return jnp.stack([real_part, imag_part])

    sent = half_product(1 - my_half)
    got = lax.ppermute(sent, "int", [(0, 1), (1, 0)])
    my_share = half_product(my_half) + got
    kept_data = filled.reshape(comp_count, freq_count, local_rows, half_count, out_cols)
    kept_data = lax.dynamic_index_in_dim(kept_data, my_half, 3, keepdims=False)
    w_real = wavelet[0][:, None, None]
    w_imag = wavelet[1][:, None, None]
    out_real = kept_data[0] - (w_real * my_share[0] - w_imag * my_share[1])
    out_imag = kept_data[1] - (w_real * my_share[1] + w_imag * my_share[0])
    return jnp.stack([out_real, out_imag])


def solution(mesh):
    placed = (P(None, None, "src", "rcv"), P("src", "rcv"), P("src", None), P())
    return jax.shard_map(
        per_device,
        mesh=mesh,
        in_specs=placed,
        out_specs=P(None, None, "src", ("rcv", "int")),
        check_vma=False,
    )
```

```python
import jax
import jax.numpy as jnp
from jax import lax
from jax.sharding import PartitionSpec as P

TILE = 128


def from_everyone(x, axis):
    copies = jnp.broadcast_to(x, (lax.axis_size(axis), *x.shape))
    return lax.all_to_all(copies, axis, split_axis=0, concat_axis=0, tiled=True)


def joined_along(pieces, dim):
    pieces = jnp.moveaxis(pieces, 0, dim)
    lengths = pieces.shape
    return pieces.reshape(*lengths[:dim], lengths[dim] * lengths[dim + 1], *lengths[dim + 2 :])


def collect(x, axis, dim):
    pieces = from_everyone(x, axis)
    return joined_along(pieces, dim)


def in_blocks(x, dim, count):
    before, after = (x.shape[:dim], x.shape[dim + 1 :])
    return jnp.moveaxis(x.reshape(*before, count, -1, *after), dim, 0)


def sent_and_summed(x, axis, dim):
    pieces = in_blocks(x, dim, lax.axis_size(axis))
    arrived = lax.all_to_all(pieces, axis, split_axis=0, concat_axis=0, tiled=True)
    return arrived.sum(axis=0)


def mirror_pairs(n_src, n_rcv, per_rcv, step):
    pairs = []
    for s in range(n_src):
        for r in range(n_rcv):
            t = (s % per_rcv + step) % per_rcv
            dest_s = per_rcv * r + t
            if s > dest_s:
                pairs.append((s * n_rcv + r, dest_s * n_rcv + s // per_rcv))
    return pairs


def complex_prod(left_side, right_side):
    return jnp.einsum("fik,fkj->fij", left_side, right_side, precision=lax.Precision.HIGHEST)


def per_device(traces, missing, aperture, wavelet):
    half_count = lax.axis_size("int")
    my_half = lax.axis_index("int")
    rcv_count = lax.axis_size("rcv")
    comp_count, freq_count, local_rows, local_cols = traces.shape
    per_rcv = local_cols // TILE
    src_count = lax.axis_size("src")
    me_src = lax.axis_index("src")
    tiles = traces.reshape(comp_count, freq_count, TILE, per_rcv, TILE)
    arrived = []
    for step in range(per_rcv):
        pick = (me_src % per_rcv + step) % per_rcv
        sent = lax.dynamic_index_in_dim(tiles, pick, 3, keepdims=False)
        got = lax.ppermute(sent, ("src", "rcv"), mirror_pairs(src_count, rcv_count, per_rcv, step))
        arrived.append(jnp.swapaxes(got, 2, 3))
    arrived = jnp.stack(arrived, axis=3)
    order = (me_src % per_rcv - jnp.arange(per_rcv)) % per_rcv
    mirrored = jnp.take(arrived, order, axis=3)
    marks = (missing[0] > 0)[None, None, None, :, None]
    filled = jnp.where(marks, mirrored, tiles).reshape(traces.shape)
    row_tiles = local_rows // TILE
    col_tiles = local_cols // TILE
    half_tile = TILE // half_count
    left_half = filled.reshape(comp_count, freq_count, local_rows, col_tiles, half_count, half_tile)
    left_half = lax.dynamic_index_in_dim(left_half, my_half, 4, keepdims=False)
    left_half = left_half.reshape(comp_count, freq_count, local_rows, col_tiles * half_tile)
    out_cols = local_cols // half_count
    right_half = filled.reshape(comp_count, freq_count, row_tiles, half_count, half_tile, half_count, out_cols)
    right_half = lax.dynamic_index_in_dim(right_half, my_half, 3, keepdims=False)
    right_half = jnp.transpose(right_half, (4, 0, 1, 2, 3, 5))
    right_half = right_half.reshape(half_count, comp_count, freq_count, row_tiles * half_tile, out_cols)
    gathered = collect(left_half, "rcv", 3)
    block_count = gathered.shape[3] // half_tile
    chosen = (
        (aperture[:, :, None] == jnp.arange(block_count, dtype=jnp.int32)[None, None, :])
        .astype(jnp.float32)
        .sum(axis=1)
    )
    weighted = gathered.reshape(comp_count, freq_count, row_tiles, TILE, block_count, half_tile)
    weighted = (weighted * chosen[None, None, :, None, :, None]).reshape(
        comp_count, freq_count, local_rows, block_count * half_tile
    )
    assert half_count == 2

    def half_product(which):
        piece = lax.dynamic_index_in_dim(right_half, which, 0, keepdims=False)
        cols = lax.all_gather(piece, "src", axis=2, tiled=True)
        real_part = complex_prod(weighted[0], cols[0]) - complex_prod(weighted[1], cols[1])
        imag_part = complex_prod(weighted[0], cols[1]) + complex_prod(weighted[1], cols[0])
        return jnp.stack([real_part, imag_part])

    sent = half_product(1 - my_half)
    got = lax.ppermute(sent, "int", [(0, 1), (1, 0)])
    my_share = half_product(my_half) + got
    kept_data = filled.reshape(comp_count, freq_count, local_rows, half_count, out_cols)
    kept_data = lax.dynamic_index_in_dim(kept_data, my_half, 3, keepdims=False)
    w_real = wavelet[0][:, None, None]
    w_imag = wavelet[1][:, None, None]
    out_real = kept_data[0] - (w_real * my_share[0] - w_imag * my_share[1])
    out_imag = kept_data[1] - (w_real * my_share[1] + w_imag * my_share[0])
    return jnp.stack([out_real, out_imag])


def solution(mesh):
    placed = (P(None, None, "src", "rcv"), P("src", "rcv"), P("src", None), P())
    return jax.shard_map(
        per_device,
        mesh=mesh,
        in_specs=placed,
        out_specs=P(None, None, "src", ("rcv", "int")),
        check_vma=False,
    )
```

```python
import jax
import jax.numpy as jnp
from jax import lax
from jax.sharding import PartitionSpec as P

TILE = 128


def from_everyone(x, axis):
    copies = jnp.broadcast_to(x, (lax.axis_size(axis), *x.shape))
    return lax.all_to_all(copies, axis, split_axis=0, concat_axis=0, tiled=True)


def joined_along(pieces, dim):
    pieces = jnp.moveaxis(pieces, 0, dim)
    lengths = pieces.shape
    return pieces.reshape(*lengths[:dim], lengths[dim] * lengths[dim + 1], *lengths[dim + 2 :])


def collect(x, axis, dim):
    pieces = from_everyone(x, axis)
    return joined_along(pieces, dim)


def in_blocks(x, dim, count):
    before, after = (x.shape[:dim], x.shape[dim + 1 :])
    return jnp.moveaxis(x.reshape(*before, count, -1, *after), dim, 0)


def sent_and_summed(x, axis, dim):
    pieces = in_blocks(x, dim, lax.axis_size(axis))
    arrived = lax.all_to_all(pieces, axis, split_axis=0, concat_axis=0, tiled=True)
    return arrived.sum(axis=0)


def mirror_pairs(n_src, n_rcv, per_rcv, step):
    pairs = []
    for s in range(n_src):
        for r in range(n_rcv):
            t = (s % per_rcv + step) % per_rcv
            dest_s = per_rcv * r + t
            if s > dest_s:
                pairs.append((s * n_rcv + r, dest_s * n_rcv + s // per_rcv))
    return pairs


def complex_prod(left_side, right_side):
    return jnp.einsum("fik,fkj->fij", left_side, right_side, precision=lax.Precision.HIGH)


def per_device(traces, missing, aperture, wavelet):
    half_count = lax.axis_size("int")
    my_half = lax.axis_index("int")
    rcv_count = lax.axis_size("rcv")
    comp_count, freq_count, local_rows, local_cols = traces.shape
    per_rcv = local_cols // TILE
    src_count = lax.axis_size("src")
    me_src = lax.axis_index("src")
    tiles = traces.reshape(comp_count, freq_count, TILE, per_rcv, TILE)
    arrived = []
    for step in range(per_rcv):
        pick = (me_src % per_rcv + step) % per_rcv
        sent = lax.dynamic_index_in_dim(tiles, pick, 3, keepdims=False)
        got = lax.ppermute(sent, ("src", "rcv"), mirror_pairs(src_count, rcv_count, per_rcv, step))
        arrived.append(jnp.swapaxes(got, 2, 3))
    arrived = jnp.stack(arrived, axis=3)
    order = (me_src % per_rcv - jnp.arange(per_rcv)) % per_rcv
    mirrored = jnp.take(arrived, order, axis=3)
    marks = (missing[0] > 0)[None, None, None, :, None]
    filled = jnp.where(marks, mirrored, tiles).reshape(traces.shape)
    row_tiles = local_rows // TILE
    col_tiles = local_cols // TILE
    half_tile = TILE // half_count
    left_half = filled.reshape(comp_count, freq_count, local_rows, col_tiles, half_count, half_tile)
    left_half = lax.dynamic_index_in_dim(left_half, my_half, 4, keepdims=False)
    left_half = left_half.reshape(comp_count, freq_count, local_rows, col_tiles * half_tile)
    right_half = filled.reshape(
        comp_count, freq_count, row_tiles, half_count, half_tile, local_cols
    )
    right_half = lax.dynamic_index_in_dim(right_half, my_half, 3, keepdims=False)
    right_half = right_half.reshape(comp_count, freq_count, row_tiles * half_tile, local_cols)
    gathered = collect(left_half, "rcv", 3)
    block_count = gathered.shape[3] // half_tile
    chosen = (
        (aperture[:, :, None] == jnp.arange(block_count, dtype=jnp.int32)[None, None, :])
        .astype(jnp.float32)
        .sum(axis=1)
    )
    weighted = gathered.reshape(comp_count, freq_count, row_tiles, TILE, block_count, half_tile)
    weighted = (weighted * chosen[None, None, :, None, :, None]).reshape(
        comp_count, freq_count, local_rows, block_count * half_tile
    )
    slab_piece = lax.all_gather(right_half, "src", axis=2, tiled=True)
    real_part = complex_prod(weighted[0], slab_piece[0]) - complex_prod(weighted[1], slab_piece[1])
    imag_part = complex_prod(weighted[0], slab_piece[1]) + complex_prod(weighted[1], slab_piece[0])
    partial_sum = jnp.stack([real_part, imag_part])
    out_cols = local_cols // half_count
    my_share = sent_and_summed(partial_sum, "int", 3)
    kept_data = filled.reshape(comp_count, freq_count, local_rows, half_count, out_cols)
    kept_data = lax.dynamic_index_in_dim(kept_data, my_half, 3, keepdims=False)
    w_real = wavelet[0][:, None, None]
    w_imag = wavelet[1][:, None, None]
    out_real = kept_data[0] - (w_real * my_share[0] - w_imag * my_share[1])
    out_imag = kept_data[1] - (w_real * my_share[1] + w_imag * my_share[0])
    return jnp.stack([out_real, out_imag])


def solution(mesh):
    placed = (P(None, None, "src", "rcv"), P("src", "rcv"), P("src", None), P())
    return jax.shard_map(
        per_device,
        mesh=mesh,
        in_specs=placed,
        out_specs=P(None, None, "src", ("rcv", "int")),
        check_vma=False,
    )
```

```python
import jax
import jax.numpy as jnp
from jax import lax
from jax.sharding import PartitionSpec as P

TILE = 128


def from_everyone(x, axis):
    copies = jnp.broadcast_to(x, (lax.axis_size(axis), *x.shape))
    return lax.all_to_all(copies, axis, split_axis=0, concat_axis=0, tiled=True)


def joined_along(pieces, dim):
    pieces = jnp.moveaxis(pieces, 0, dim)
    lengths = pieces.shape
    return pieces.reshape(*lengths[:dim], lengths[dim] * lengths[dim + 1], *lengths[dim + 2 :])


def collect(x, axis, dim):
    pieces = from_everyone(x, axis)
    return joined_along(pieces, dim)


def in_blocks(x, dim, count):
    before, after = (x.shape[:dim], x.shape[dim + 1 :])
    return jnp.moveaxis(x.reshape(*before, count, -1, *after), dim, 0)


def sent_and_summed(x, axis, dim):
    pieces = in_blocks(x, dim, lax.axis_size(axis))
    arrived = lax.all_to_all(pieces, axis, split_axis=0, concat_axis=0, tiled=True)
    return arrived.sum(axis=0)


def mirror_pairs(n_src, n_rcv, per_rcv, step):
    pairs = []
    for s in range(n_src):
        for r in range(n_rcv):
            t = (s % per_rcv + step) % per_rcv
            dest_s = per_rcv * r + t
            if s > dest_s:
                pairs.append((s * n_rcv + r, dest_s * n_rcv + s // per_rcv))
    return pairs


def complex_prod(left_side, right_side):
    return jnp.einsum("fik,fkj->fij", left_side, right_side, precision=lax.Precision.HIGH)


def per_device(traces, missing, aperture, wavelet):
    half_count = lax.axis_size("int")
    my_half = lax.axis_index("int")
    rcv_count = lax.axis_size("rcv")
    comp_count, freq_count, local_rows, local_cols = traces.shape
    per_rcv = local_cols // TILE
    src_count = lax.axis_size("src")
    me_src = lax.axis_index("src")
    tiles = traces.reshape(comp_count, freq_count, TILE, per_rcv, TILE)
    arrived = []
    for step in range(per_rcv):
        pick = (me_src % per_rcv + step) % per_rcv
        sent = lax.dynamic_index_in_dim(tiles, pick, 3, keepdims=False)
        got = lax.ppermute(sent, ("src", "rcv"), mirror_pairs(src_count, rcv_count, per_rcv, step))
        arrived.append(jnp.swapaxes(got, 2, 3))
    arrived = jnp.stack(arrived, axis=3)
    order = (me_src % per_rcv - jnp.arange(per_rcv)) % per_rcv
    mirrored = jnp.take(arrived, order, axis=3)
    marks = (missing[0] > 0)[None, None, None, :, None]
    filled = jnp.where(marks, mirrored, tiles).reshape(traces.shape)
    row_tiles = local_rows // TILE
    col_tiles = local_cols // TILE
    half_tile = TILE // half_count
    left_half = filled.reshape(comp_count, freq_count, local_rows, col_tiles, half_count, half_tile)
    left_half = lax.dynamic_index_in_dim(left_half, my_half, 4, keepdims=False)
    left_half = left_half.reshape(comp_count, freq_count, local_rows, col_tiles * half_tile)
    right_half = filled.reshape(
        comp_count, freq_count, row_tiles, half_count, half_tile, local_cols
    )
    right_half = lax.dynamic_index_in_dim(right_half, my_half, 3, keepdims=False)
    right_half = right_half.reshape(comp_count, freq_count, row_tiles * half_tile, local_cols)
    gathered = collect(left_half, "rcv", 3)
    block_count = gathered.shape[3] // half_tile
    chosen = (
        (aperture[:, :, None] == jnp.arange(block_count, dtype=jnp.int32)[None, None, :])
        .astype(jnp.float32)
        .sum(axis=1)
    )
    weighted = gathered.reshape(comp_count, freq_count, row_tiles, TILE, block_count, half_tile)
    weighted = (weighted * chosen[None, None, :, None, :, None]).reshape(
        comp_count, freq_count, local_rows, block_count * half_tile
    )
    slab_piece = lax.all_gather(right_half, "src", axis=2, tiled=True)
    out_cols = local_cols // half_count
    assert half_count == 2

    def half_product(which):
        cols = lax.dynamic_slice_in_dim(slab_piece, which * out_cols, out_cols, axis=3)
        real_part = complex_prod(weighted[0], cols[0]) - complex_prod(weighted[1], cols[1])
        imag_part = complex_prod(weighted[0], cols[1]) + complex_prod(weighted[1], cols[0])
        return jnp.stack([real_part, imag_part])

    sent = half_product(1 - my_half)
    got = lax.ppermute(sent, "int", [(0, 1), (1, 0)])
    my_share = half_product(my_half) + got
    kept_data = filled.reshape(comp_count, freq_count, local_rows, half_count, out_cols)
    kept_data = lax.dynamic_index_in_dim(kept_data, my_half, 3, keepdims=False)
    w_real = wavelet[0][:, None, None]
    w_imag = wavelet[1][:, None, None]
    out_real = kept_data[0] - (w_real * my_share[0] - w_imag * my_share[1])
    out_imag = kept_data[1] - (w_real * my_share[1] + w_imag * my_share[0])
    return jnp.stack([out_real, out_imag])


def solution(mesh):
    placed = (P(None, None, "src", "rcv"), P("src", "rcv"), P("src", None), P())
    return jax.shard_map(
        per_device,
        mesh=mesh,
        in_specs=placed,
        out_specs=P(None, None, "src", ("rcv", "int")),
        check_vma=False,
    )
```

```python
import jax
import jax.numpy as jnp
from jax import lax
from jax.sharding import PartitionSpec as P

TILE = 128


def from_everyone(x, axis):
    copies = jnp.broadcast_to(x, (lax.axis_size(axis), *x.shape))
    return lax.all_to_all(copies, axis, split_axis=0, concat_axis=0, tiled=True)


def joined_along(pieces, dim):
    pieces = jnp.moveaxis(pieces, 0, dim)
    lengths = pieces.shape
    return pieces.reshape(*lengths[:dim], lengths[dim] * lengths[dim + 1], *lengths[dim + 2 :])


def collect(x, axis, dim):
    pieces = from_everyone(x, axis)
    return joined_along(pieces, dim)


def in_blocks(x, dim, count):
    before, after = (x.shape[:dim], x.shape[dim + 1 :])
    return jnp.moveaxis(x.reshape(*before, count, -1, *after), dim, 0)


def sent_and_summed(x, axis, dim):
    pieces = in_blocks(x, dim, lax.axis_size(axis))
    arrived = lax.all_to_all(pieces, axis, split_axis=0, concat_axis=0, tiled=True)
    return arrived.sum(axis=0)


def mirror_pairs(n_src, n_rcv, per_rcv, step):
    pairs = []
    for s in range(n_src):
        for r in range(n_rcv):
            t = (s % per_rcv + step) % per_rcv
            dest_s = per_rcv * r + t
            if s > dest_s:
                pairs.append((s * n_rcv + r, dest_s * n_rcv + s // per_rcv))
    return pairs


def complex_prod(left_side, right_side):
    return jnp.einsum("fik,fkj->fij", left_side, right_side, precision=lax.Precision.HIGH)


def per_device(traces, missing, aperture, wavelet):
    half_count = lax.axis_size("int")
    my_half = lax.axis_index("int")
    rcv_count = lax.axis_size("rcv")
    comp_count, freq_count, local_rows, local_cols = traces.shape
    per_rcv = local_cols // TILE
    src_count = lax.axis_size("src")
    me_src = lax.axis_index("src")
    tiles = traces.reshape(comp_count, freq_count, TILE, per_rcv, TILE)
    assert comp_count == half_count
    arrived = []
    for step in range(per_rcv):
        pick = (me_src % per_rcv + step) % per_rcv
        sent = lax.dynamic_index_in_dim(tiles, pick, 3, keepdims=False)
        sent = lax.dynamic_index_in_dim(sent, my_half, 0, keepdims=False)
        got = lax.ppermute(sent, ("src", "rcv"), mirror_pairs(src_count, rcv_count, per_rcv, step))
        arrived.append(jnp.swapaxes(got, 1, 2))
    mine = jnp.stack(arrived, axis=2)
    theirs = lax.ppermute(mine, "int", [(0, 1), (1, 0)])
    arrived = jnp.stack([mine, theirs])
    arrived = jnp.take(arrived, (jnp.arange(comp_count) + my_half) % comp_count, axis=0)
    order = (me_src % per_rcv - jnp.arange(per_rcv)) % per_rcv
    mirrored = jnp.take(arrived, order, axis=3)
    marks = (missing[0] > 0)[None, None, None, :, None]
    filled = jnp.where(marks, mirrored, tiles).reshape(traces.shape)
    row_tiles = local_rows // TILE
    col_tiles = local_cols // TILE
    half_tile = TILE // half_count
    left_half = filled.reshape(comp_count, freq_count, local_rows, col_tiles, half_count, half_tile)
    left_half = lax.dynamic_index_in_dim(left_half, my_half, 4, keepdims=False)
    left_half = left_half.reshape(comp_count, freq_count, local_rows, col_tiles * half_tile)
    right_half = filled.reshape(
        comp_count, freq_count, row_tiles, half_count, half_tile, local_cols
    )
    right_half = lax.dynamic_index_in_dim(right_half, my_half, 3, keepdims=False)
    right_half = right_half.reshape(comp_count, freq_count, row_tiles * half_tile, local_cols)
    gathered = collect(left_half, "rcv", 3)
    block_count = gathered.shape[3] // half_tile
    chosen = (
        (aperture[:, :, None] == jnp.arange(block_count, dtype=jnp.int32)[None, None, :])
        .astype(jnp.float32)
        .sum(axis=1)
    )
    weighted = gathered.reshape(comp_count, freq_count, row_tiles, TILE, block_count, half_tile)
    weighted = (weighted * chosen[None, None, :, None, :, None]).reshape(
        comp_count, freq_count, local_rows, block_count * half_tile
    )
    slab_piece = lax.all_gather(right_half, "src", axis=2, tiled=True)
    out_cols = local_cols // half_count
    assert half_count == 2

    def half_product(which):
        cols = lax.dynamic_slice_in_dim(slab_piece, which * out_cols, out_cols, axis=3)
        real_part = complex_prod(weighted[0], cols[0]) - complex_prod(weighted[1], cols[1])
        imag_part = complex_prod(weighted[0], cols[1]) + complex_prod(weighted[1], cols[0])
        return jnp.stack([real_part, imag_part])

    sent = half_product(1 - my_half)
    got = lax.ppermute(sent, "int", [(0, 1), (1, 0)])
    my_share = half_product(my_half) + got
    kept_data = filled.reshape(comp_count, freq_count, local_rows, half_count, out_cols)
    kept_data = lax.dynamic_index_in_dim(kept_data, my_half, 3, keepdims=False)
    w_real = wavelet[0][:, None, None]
    w_imag = wavelet[1][:, None, None]
    out_real = kept_data[0] - (w_real * my_share[0] - w_imag * my_share[1])
    out_imag = kept_data[1] - (w_real * my_share[1] + w_imag * my_share[0])
    return jnp.stack([out_real, out_imag])


def solution(mesh):
    placed = (P(None, None, "src", "rcv"), P("src", "rcv"), P("src", None), P())
    return jax.shard_map(
        per_device,
        mesh=mesh,
        in_specs=placed,
        out_specs=P(None, None, "src", ("rcv", "int")),
        check_vma=False,
    )
```

```python
import jax
import jax.numpy as jnp
from jax import lax
from jax.sharding import PartitionSpec as P

TILE = 128


def from_everyone(x, axis):
    copies = jnp.broadcast_to(x, (lax.axis_size(axis), *x.shape))
    return lax.all_to_all(copies, axis, split_axis=0, concat_axis=0, tiled=True)


def joined_along(pieces, dim):
    pieces = jnp.moveaxis(pieces, 0, dim)
    lengths = pieces.shape
    return pieces.reshape(*lengths[:dim], lengths[dim] * lengths[dim + 1], *lengths[dim + 2 :])


def collect(x, axis, dim):
    pieces = from_everyone(x, axis)
    return joined_along(pieces, dim)


def in_blocks(x, dim, count):
    before, after = (x.shape[:dim], x.shape[dim + 1 :])
    return jnp.moveaxis(x.reshape(*before, count, -1, *after), dim, 0)


def sent_and_summed(x, axis, dim):
    pieces = in_blocks(x, dim, lax.axis_size(axis))
    arrived = lax.all_to_all(pieces, axis, split_axis=0, concat_axis=0, tiled=True)
    return arrived.sum(axis=0)


def mirror_pairs(n_src, n_rcv, per_rcv, step):
    pairs = []
    for s in range(n_src):
        for r in range(n_rcv):
            t = (s % per_rcv + step) % per_rcv
            dest_s = per_rcv * r + t
            if s > dest_s:
                pairs.append((s * n_rcv + r, dest_s * n_rcv + s // per_rcv))
    return pairs


def complex_prod(left_side, right_side):
    return jnp.einsum("fik,fkj->fij", left_side, right_side, precision=lax.Precision.HIGH)


def per_device(traces, missing, aperture, wavelet):
    half_count = lax.axis_size("int")
    my_half = lax.axis_index("int")
    rcv_count = lax.axis_size("rcv")
    comp_count, freq_count, local_rows, local_cols = traces.shape
    per_rcv = local_cols // TILE
    src_count = lax.axis_size("src")
    me_src = lax.axis_index("src")
    tiles = traces.reshape(comp_count, freq_count, TILE, per_rcv, TILE)
    assert comp_count == half_count
    mine, theirs = [], []
    for step in range(per_rcv):
        pick = (me_src % per_rcv + step) % per_rcv
        sent = lax.dynamic_index_in_dim(tiles, pick, 3, keepdims=False)
        sent = lax.dynamic_index_in_dim(sent, my_half, 0, keepdims=False)
        got = lax.ppermute(sent, ("src", "rcv"), mirror_pairs(src_count, rcv_count, per_rcv, step))
        mine.append(jnp.swapaxes(got, 1, 2))
        theirs.append(jnp.swapaxes(lax.ppermute(got, "int", [(0, 1), (1, 0)]), 1, 2))
    arrived = jnp.stack([jnp.stack(mine, axis=2), jnp.stack(theirs, axis=2)])
    arrived = jnp.take(arrived, (jnp.arange(comp_count) + my_half) % comp_count, axis=0)
    order = (me_src % per_rcv - jnp.arange(per_rcv)) % per_rcv
    mirrored = jnp.take(arrived, order, axis=3)
    marks = (missing[0] > 0)[None, None, None, :, None]
    filled = jnp.where(marks, mirrored, tiles).reshape(traces.shape)
    row_tiles = local_rows // TILE
    col_tiles = local_cols // TILE
    half_tile = TILE // half_count
    left_half = filled.reshape(comp_count, freq_count, local_rows, col_tiles, half_count, half_tile)
    left_half = lax.dynamic_index_in_dim(left_half, my_half, 4, keepdims=False)
    left_half = left_half.reshape(comp_count, freq_count, local_rows, col_tiles * half_tile)
    right_half = filled.reshape(
        comp_count, freq_count, row_tiles, half_count, half_tile, local_cols
    )
    right_half = lax.dynamic_index_in_dim(right_half, my_half, 3, keepdims=False)
    right_half = right_half.reshape(comp_count, freq_count, row_tiles * half_tile, local_cols)
    gathered = collect(left_half, "rcv", 3)
    block_count = gathered.shape[3] // half_tile
    chosen = (
        (aperture[:, :, None] == jnp.arange(block_count, dtype=jnp.int32)[None, None, :])
        .astype(jnp.float32)
        .sum(axis=1)
    )
    weighted = gathered.reshape(comp_count, freq_count, row_tiles, TILE, block_count, half_tile)
    weighted = (weighted * chosen[None, None, :, None, :, None]).reshape(
        comp_count, freq_count, local_rows, block_count * half_tile
    )
    slab_piece = lax.all_gather(right_half, "src", axis=2, tiled=True)
    out_cols = local_cols // half_count
    assert half_count == 2

    def half_product(which):
        cols = lax.dynamic_slice_in_dim(slab_piece, which * out_cols, out_cols, axis=3)
        real_part = complex_prod(weighted[0], cols[0]) - complex_prod(weighted[1], cols[1])
        imag_part = complex_prod(weighted[0], cols[1]) + complex_prod(weighted[1], cols[0])
        return jnp.stack([real_part, imag_part])

    sent = half_product(1 - my_half)
    got = lax.ppermute(sent, "int", [(0, 1), (1, 0)])
    my_share = half_product(my_half) + got
    kept_data = filled.reshape(comp_count, freq_count, local_rows, half_count, out_cols)
    kept_data = lax.dynamic_index_in_dim(kept_data, my_half, 3, keepdims=False)
    w_real = wavelet[0][:, None, None]
    w_imag = wavelet[1][:, None, None]
    out_real = kept_data[0] - (w_real * my_share[0] - w_imag * my_share[1])
    out_imag = kept_data[1] - (w_real * my_share[1] + w_imag * my_share[0])
    return jnp.stack([out_real, out_imag])


def solution(mesh):
    placed = (P(None, None, "src", "rcv"), P("src", "rcv"), P("src", None), P())
    return jax.shard_map(
        per_device,
        mesh=mesh,
        in_specs=placed,
        out_specs=P(None, None, "src", ("rcv", "int")),
        check_vma=False,
    )
```

```python
import jax
import jax.numpy as jnp
from jax import lax
from jax.sharding import PartitionSpec as P

TILE = 128


def from_everyone(x, axis):
    copies = jnp.broadcast_to(x, (lax.axis_size(axis), *x.shape))
    return lax.all_to_all(copies, axis, split_axis=0, concat_axis=0, tiled=True)


def joined_along(pieces, dim):
    pieces = jnp.moveaxis(pieces, 0, dim)
    lengths = pieces.shape
    return pieces.reshape(*lengths[:dim], lengths[dim] * lengths[dim + 1], *lengths[dim + 2 :])


def collect(x, axis, dim):
    pieces = from_everyone(x, axis)
    return joined_along(pieces, dim)


def in_blocks(x, dim, count):
    before, after = (x.shape[:dim], x.shape[dim + 1 :])
    return jnp.moveaxis(x.reshape(*before, count, -1, *after), dim, 0)


def sent_and_summed(x, axis, dim):
    pieces = in_blocks(x, dim, lax.axis_size(axis))
    arrived = lax.all_to_all(pieces, axis, split_axis=0, concat_axis=0, tiled=True)
    return arrived.sum(axis=0)


def mirror_pairs(n_src, n_rcv, per_rcv, step):
    pairs = []
    for s in range(n_src):
        for r in range(n_rcv):
            t = (s % per_rcv + step) % per_rcv
            dest_s = per_rcv * r + t
            if s > dest_s:
                pairs.append((s * n_rcv + r, dest_s * n_rcv + s // per_rcv))
    return pairs


def complex_prod(left_side, right_side):
    return jnp.einsum("fik,fkj->fij", left_side, right_side, precision=lax.Precision.HIGH)


def per_device(traces, missing, aperture, wavelet):
    half_count = lax.axis_size("int")
    my_half = lax.axis_index("int")
    rcv_count = lax.axis_size("rcv")
    comp_count, freq_count, local_rows, local_cols = traces.shape
    per_rcv = local_cols // TILE
    src_count = lax.axis_size("src")
    me_src = lax.axis_index("src")
    tiles = traces.reshape(comp_count, freq_count, TILE, per_rcv, TILE)
    assert comp_count == half_count
    arrived = []
    for step in range(per_rcv):
        pick = (me_src % per_rcv + step) % per_rcv
        sent = lax.dynamic_index_in_dim(tiles, pick, 3, keepdims=False)
        sent = lax.dynamic_index_in_dim(sent, my_half, 0, keepdims=False)
        got = lax.ppermute(sent, ("src", "rcv"), mirror_pairs(src_count, rcv_count, per_rcv, step))
        arrived.append(jnp.swapaxes(got, 1, 2))
    mine = jnp.stack(arrived, axis=2)
    theirs = lax.ppermute(mine, "int", [(0, 1), (1, 0)])
    arrived = jnp.stack([mine, theirs])
    arrived = jnp.take(arrived, (jnp.arange(comp_count) + my_half) % comp_count, axis=0)
    order = (me_src % per_rcv - jnp.arange(per_rcv)) % per_rcv
    mirrored = jnp.take(arrived, order, axis=3)
    marks = (missing[0] > 0)[None, None, None, :, None]
    filled = jnp.where(marks, mirrored, tiles).reshape(traces.shape)
    row_tiles = local_rows // TILE
    col_tiles = local_cols // TILE
    half_tile = TILE // half_count
    left_half = filled.reshape(comp_count, freq_count, local_rows, col_tiles, half_count, half_tile)
    left_half = lax.dynamic_index_in_dim(left_half, my_half, 4, keepdims=False)
    left_half = left_half.reshape(comp_count, freq_count, local_rows, col_tiles * half_tile)
    right_half = filled.reshape(
        comp_count, freq_count, row_tiles, half_count, half_tile, local_cols
    )
    right_half = lax.dynamic_index_in_dim(right_half, my_half, 3, keepdims=False)
    right_half = right_half.reshape(comp_count, freq_count, row_tiles * half_tile, local_cols)
    gathered = collect(left_half, "rcv", 3)
    block_count = gathered.shape[3] // half_tile
    chosen = (
        (aperture[:, :, None] == jnp.arange(block_count, dtype=jnp.int32)[None, None, :])
        .astype(jnp.float32)
        .sum(axis=1)
    )
    weighted = gathered.reshape(comp_count, freq_count, row_tiles, TILE, block_count, half_tile)
    weighted = (weighted * chosen[None, None, :, None, :, None]).reshape(
        comp_count, freq_count, local_rows, block_count * half_tile
    )
    slab_piece = jnp.transpose(right_half, (1, 2, 0, 3)).reshape(
        freq_count, row_tiles * half_tile, comp_count * local_cols
    )
    slab_piece = lax.all_gather(slab_piece, "src", axis=1, tiled=True)
    out_cols = local_cols // half_count
    assert half_count == 2

    def half_product(which):
        cols = [
            lax.dynamic_slice_in_dim(slab_piece, comp * local_cols + which * out_cols, out_cols, axis=2)
            for comp in range(comp_count)
        ]
        real_part = complex_prod(weighted[0], cols[0]) - complex_prod(weighted[1], cols[1])
        imag_part = complex_prod(weighted[0], cols[1]) + complex_prod(weighted[1], cols[0])
        return jnp.stack([real_part, imag_part])

    sent = half_product(1 - my_half)
    got = lax.ppermute(sent, "int", [(0, 1), (1, 0)])
    my_share = half_product(my_half) + got
    kept_data = filled.reshape(comp_count, freq_count, local_rows, half_count, out_cols)
    kept_data = lax.dynamic_index_in_dim(kept_data, my_half, 3, keepdims=False)
    w_real = wavelet[0][:, None, None]
    w_imag = wavelet[1][:, None, None]
    out_real = kept_data[0] - (w_real * my_share[0] - w_imag * my_share[1])
    out_imag = kept_data[1] - (w_real * my_share[1] + w_imag * my_share[0])
    return jnp.stack([out_real, out_imag])


def solution(mesh):
    placed = (P(None, None, "src", "rcv"), P("src", "rcv"), P("src", None), P())
    return jax.shard_map(
        per_device,
        mesh=mesh,
        in_specs=placed,
        out_specs=P(None, None, "src", ("rcv", "int")),
        check_vma=False,
    )
```

```python
import jax
import jax.numpy as jnp
from jax import lax
from jax.sharding import PartitionSpec as P

TILE = 128


def from_everyone(x, axis):
    copies = jnp.broadcast_to(x, (lax.axis_size(axis), *x.shape))
    return lax.all_to_all(copies, axis, split_axis=0, concat_axis=0, tiled=True)


def joined_along(pieces, dim):
    pieces = jnp.moveaxis(pieces, 0, dim)
    lengths = pieces.shape
    return pieces.reshape(*lengths[:dim], lengths[dim] * lengths[dim + 1], *lengths[dim + 2 :])


def collect(x, axis, dim):
    pieces = from_everyone(x, axis)
    return joined_along(pieces, dim)


def in_blocks(x, dim, count):
    before, after = (x.shape[:dim], x.shape[dim + 1 :])
    return jnp.moveaxis(x.reshape(*before, count, -1, *after), dim, 0)


def sent_and_summed(x, axis, dim):
    pieces = in_blocks(x, dim, lax.axis_size(axis))
    arrived = lax.all_to_all(pieces, axis, split_axis=0, concat_axis=0, tiled=True)
    return arrived.sum(axis=0)


def mirror_pairs(n_src, n_rcv, per_rcv, step):
    pairs = []
    for s in range(n_src):
        for r in range(n_rcv):
            t = (s % per_rcv + step) % per_rcv
            dest_s = per_rcv * r + t
            if s > dest_s:
                pairs.append((s * n_rcv + r, dest_s * n_rcv + s // per_rcv))
    return pairs


def block_pairs(n_src, n_rcv, per_rcv):
    pairs = []
    for s in range(n_src):
        for r in range(n_rcv):
            if s > per_rcv * r:
                pairs.append((s * n_rcv + r, (per_rcv * r + s % per_rcv) * n_rcv + s // per_rcv))
    return pairs


def trade_pairs(n_src, n_rcv, per_rcv, dist):
    pairs = []
    for q in range(n_src // per_rcv):
        for u in range(per_rcv):
            t = u ^ dist
            for r in range(n_rcv):
                if per_rcv * r + u > per_rcv * q + t:
                    pairs.append(((per_rcv * q + u) * n_rcv + r, (per_rcv * q + t) * n_rcv + r))
    return pairs


def complex_prod(left_side, right_side):
    return jnp.einsum("fik,fkj->fij", left_side, right_side, precision=lax.Precision.HIGH)


def per_device(traces, missing, aperture, wavelet):
    half_count = lax.axis_size("int")
    my_half = lax.axis_index("int")
    rcv_count = lax.axis_size("rcv")
    comp_count, freq_count, local_rows, local_cols = traces.shape
    per_rcv = local_cols // TILE
    src_count = lax.axis_size("src")
    me_src = lax.axis_index("src")
    tiles = traces.reshape(comp_count, freq_count, TILE, per_rcv, TILE)
    assert comp_count == half_count
    own = lax.dynamic_index_in_dim(tiles, my_half, 0, keepdims=False)
    held = lax.ppermute(own, ("src", "rcv"), block_pairs(src_count, rcv_count, per_rcv))
    slot = me_src % per_rcv
    pieces = []
    for dist in range(per_rcv):
        piece = lax.dynamic_index_in_dim(held, slot ^ dist, 2, keepdims=False)
        if dist:
            piece = lax.ppermute(piece, ("src", "rcv"), trade_pairs(src_count, rcv_count, per_rcv, dist))
        pieces.append(piece)
    pieces = jnp.stack(pieces, axis=2)
    mine = jnp.take(pieces, jnp.arange(per_rcv) ^ slot, axis=2)
    mine = jnp.swapaxes(mine, 1, 3)
    theirs = lax.ppermute(mine, "int", [(0, 1), (1, 0)])
    mirrored = jnp.stack([mine, theirs])
    mirrored = jnp.take(mirrored, (jnp.arange(comp_count) + my_half) % comp_count, axis=0)
    marks = (missing[0] > 0)[None, None, None, :, None]
    filled = jnp.where(marks, mirrored, tiles).reshape(traces.shape)
    row_tiles = local_rows // TILE
    col_tiles = local_cols // TILE
    half_tile = TILE // half_count
    left_half = filled.reshape(comp_count, freq_count, local_rows, col_tiles, half_count, half_tile)
    left_half = lax.dynamic_index_in_dim(left_half, my_half, 4, keepdims=False)
    left_half = left_half.reshape(comp_count, freq_count, local_rows, col_tiles * half_tile)
    right_half = filled.reshape(
        comp_count, freq_count, row_tiles, half_count, half_tile, local_cols
    )
    right_half = lax.dynamic_index_in_dim(right_half, my_half, 3, keepdims=False)
    right_half = right_half.reshape(comp_count, freq_count, row_tiles * half_tile, local_cols)
    gathered = collect(left_half, "rcv", 3)
    block_count = gathered.shape[3] // half_tile
    chosen = (
        (aperture[:, :, None] == jnp.arange(block_count, dtype=jnp.int32)[None, None, :])
        .astype(jnp.float32)
        .sum(axis=1)
    )
    weighted = gathered.reshape(comp_count, freq_count, row_tiles, TILE, block_count, half_tile)
    weighted = (weighted * chosen[None, None, :, None, :, None]).reshape(
        comp_count, freq_count, local_rows, block_count * half_tile
    )
    slab_piece = jnp.transpose(right_half, (1, 2, 0, 3)).reshape(
        freq_count, row_tiles * half_tile, comp_count * local_cols
    )
    slab_piece = lax.all_gather(slab_piece, "src", axis=1, tiled=True)
    out_cols = local_cols // half_count
    assert half_count == 2

    def half_product(which):
        cols = [
            lax.dynamic_slice_in_dim(slab_piece, comp * local_cols + which * out_cols, out_cols, axis=2)
            for comp in range(comp_count)
        ]
        real_part = complex_prod(weighted[0], cols[0]) - complex_prod(weighted[1], cols[1])
        imag_part = complex_prod(weighted[0], cols[1]) + complex_prod(weighted[1], cols[0])
        return jnp.stack([real_part, imag_part])

    sent = half_product(1 - my_half)
    got = lax.ppermute(sent, "int", [(0, 1), (1, 0)])
    my_share = half_product(my_half) + got
    kept_data = filled.reshape(comp_count, freq_count, local_rows, half_count, out_cols)
    kept_data = lax.dynamic_index_in_dim(kept_data, my_half, 3, keepdims=False)
    w_real = wavelet[0][:, None, None]
    w_imag = wavelet[1][:, None, None]
    out_real = kept_data[0] - (w_real * my_share[0] - w_imag * my_share[1])
    out_imag = kept_data[1] - (w_real * my_share[1] + w_imag * my_share[0])
    return jnp.stack([out_real, out_imag])


def solution(mesh):
    placed = (P(None, None, "src", "rcv"), P("src", "rcv"), P("src", None), P())
    return jax.shard_map(
        per_device,
        mesh=mesh,
        in_specs=placed,
        out_specs=P(None, None, "src", ("rcv", "int")),
        check_vma=False,
    )
```

```python
import jax
import jax.numpy as jnp
from jax import lax
from jax.sharding import PartitionSpec as P

TILE = 128


def from_everyone(x, axis):
    copies = jnp.broadcast_to(x, (lax.axis_size(axis), *x.shape))
    return lax.all_to_all(copies, axis, split_axis=0, concat_axis=0, tiled=True)


def joined_along(pieces, dim):
    pieces = jnp.moveaxis(pieces, 0, dim)
    lengths = pieces.shape
    return pieces.reshape(*lengths[:dim], lengths[dim] * lengths[dim + 1], *lengths[dim + 2 :])


def collect(x, axis, dim):
    pieces = from_everyone(x, axis)
    return joined_along(pieces, dim)


def in_blocks(x, dim, count):
    before, after = (x.shape[:dim], x.shape[dim + 1 :])
    return jnp.moveaxis(x.reshape(*before, count, -1, *after), dim, 0)


def sent_and_summed(x, axis, dim):
    pieces = in_blocks(x, dim, lax.axis_size(axis))
    arrived = lax.all_to_all(pieces, axis, split_axis=0, concat_axis=0, tiled=True)
    return arrived.sum(axis=0)


def mirror_pairs(n_src, n_rcv, per_rcv, step):
    pairs = []
    for s in range(n_src):
        for r in range(n_rcv):
            t = (s % per_rcv + step) % per_rcv
            dest_s = per_rcv * r + t
            if s > dest_s:
                pairs.append((s * n_rcv + r, dest_s * n_rcv + s // per_rcv))
    return pairs


def block_pairs(n_src, n_rcv, per_rcv):
    pairs = []
    for s in range(n_src):
        for r in range(n_rcv):
            if s > per_rcv * r:
                pairs.append((s * n_rcv + r, (per_rcv * r + s % per_rcv) * n_rcv + s // per_rcv))
    return pairs


def trade_pairs(n_src, n_rcv, per_rcv, dist):
    pairs = []
    for q in range(n_src // per_rcv):
        for u in range(per_rcv):
            t = u ^ dist
            for r in range(n_rcv):
                if per_rcv * r + u > per_rcv * q + t:
                    pairs.append(((per_rcv * q + u) * n_rcv + r, (per_rcv * q + t) * n_rcv + r))
    return pairs


def complex_prod(left_side, right_side):
    return jnp.einsum("fik,fkj->fij", left_side, right_side, precision=lax.Precision.HIGH)


def per_device(traces, missing, aperture, wavelet):
    half_count = lax.axis_size("int")
    my_half = lax.axis_index("int")
    rcv_count = lax.axis_size("rcv")
    src_count = lax.axis_size("src")
    me_src = lax.axis_index("src")
    me_rcv = lax.axis_index("rcv")
    comp_count, freq_count, local_rows, local_cols = traces.shape
    assert comp_count == half_count == 2 and local_rows == TILE
    per_rcv = local_cols // TILE
    swap = [(0, 1), (1, 0)]
    tiles = traces.reshape(comp_count, freq_count, TILE, per_rcv, TILE)
    arrived = []
    for step in range(per_rcv):
        pick = (me_src % per_rcv + step) % per_rcv
        sent = lax.dynamic_index_in_dim(tiles, pick, 3, keepdims=False)
        sent = lax.dynamic_index_in_dim(sent, my_half, 0, keepdims=False)
        got = lax.ppermute(sent, ("src", "rcv"), mirror_pairs(src_count, rcv_count, per_rcv, step))
        arrived.append(jnp.swapaxes(got, 1, 2))
    arrived = jnp.stack(arrived, axis=2)
    order = (me_src % per_rcv - jnp.arange(per_rcv)) % per_rcv
    mine = jnp.take(arrived, order, axis=2)
    marks = (missing[0] > 0)[None, None, :, None]
    own_comp = lax.dynamic_index_in_dim(tiles, my_half, 0, keepdims=False)
    filled_mine = jnp.where(marks, mine, own_comp)

    local_blocks = me_rcv * per_rcv + jnp.arange(per_rcv, dtype=jnp.int32)
    chosen = (aperture[0][:, None] == local_blocks[None, :]).astype(jnp.float32).sum(axis=0)
    left = (filled_mine * chosen[None, None, :, None]).reshape(freq_count, TILE, local_cols)
    left_mine = collect(left, "rcv", 2)
    right = lax.all_gather(filled_mine.reshape(freq_count, TILE, local_cols), "src", axis=1, tiled=True)
    left_other = lax.ppermute(left_mine, "int", swap)
    sign = jnp.where(my_half == 0, 1.0, -1.0).astype(jnp.float32)
    out_cols = local_cols // half_count

    def half_product(which):
        cols = lax.dynamic_slice_in_dim(right, which * out_cols, out_cols, axis=2)
        real_part = sign * complex_prod(left_mine, cols)
        imag_part = complex_prod(left_other, cols)
        return jnp.stack([real_part, imag_part])

    sent = half_product(1 - my_half)
    got = lax.ppermute(sent, "int", swap)
    my_share = half_product(my_half) + got

    theirs = lax.ppermute(mine, "int", swap)
    other_comp = lax.dynamic_index_in_dim(tiles, 1 - my_half, 0, keepdims=False)
    filled_other = jnp.where(marks, theirs, other_comp)
    both = jnp.stack([filled_mine, filled_other])
    both = jnp.take(both, (jnp.arange(comp_count) + my_half) % comp_count, axis=0)
    both = both.reshape(comp_count, freq_count, TILE, local_cols)
    kept_data = lax.dynamic_slice_in_dim(both, my_half * out_cols, out_cols, axis=3)
    w_real = wavelet[0][:, None, None]
    w_imag = wavelet[1][:, None, None]
    out_real = kept_data[0] - (w_real * my_share[0] - w_imag * my_share[1])
    out_imag = kept_data[1] - (w_real * my_share[1] + w_imag * my_share[0])
    return jnp.stack([out_real, out_imag])


def solution(mesh):
    placed = (P(None, None, "src", "rcv"), P("src", "rcv"), P("src", None), P())
    return jax.shard_map(
        per_device,
        mesh=mesh,
        in_specs=placed,
        out_specs=P(None, None, "src", ("rcv", "int")),
        check_vma=False,
    )
```

```python
import jax
import jax.numpy as jnp
from jax import lax
from jax.sharding import PartitionSpec as P

TILE = 128


def from_everyone(x, axis):
    copies = jnp.broadcast_to(x, (lax.axis_size(axis), *x.shape))
    return lax.all_to_all(copies, axis, split_axis=0, concat_axis=0, tiled=True)


def joined_along(pieces, dim):
    pieces = jnp.moveaxis(pieces, 0, dim)
    lengths = pieces.shape
    return pieces.reshape(*lengths[:dim], lengths[dim] * lengths[dim + 1], *lengths[dim + 2 :])


def collect(x, axis, dim):
    pieces = from_everyone(x, axis)
    return joined_along(pieces, dim)


def in_blocks(x, dim, count):
    before, after = (x.shape[:dim], x.shape[dim + 1 :])
    return jnp.moveaxis(x.reshape(*before, count, -1, *after), dim, 0)


def sent_and_summed(x, axis, dim):
    pieces = in_blocks(x, dim, lax.axis_size(axis))
    arrived = lax.all_to_all(pieces, axis, split_axis=0, concat_axis=0, tiled=True)
    return arrived.sum(axis=0)


def mirror_pairs(n_src, n_rcv, per_rcv, step):
    pairs = []
    for s in range(n_src):
        for r in range(n_rcv):
            t = (s % per_rcv + step) % per_rcv
            dest_s = per_rcv * r + t
            if s > dest_s:
                pairs.append((s * n_rcv + r, dest_s * n_rcv + s // per_rcv))
    return pairs


def complex_prod(left_side, right_side):
    return jnp.einsum("fik,fkj->fij", left_side, right_side, precision=lax.Precision.HIGH)


def per_device(traces, missing, aperture, wavelet):
    half_count = lax.axis_size("int")
    my_half = lax.axis_index("int")
    rcv_count = lax.axis_size("rcv")
    comp_count, freq_count, local_rows, local_cols = traces.shape
    per_rcv = local_cols // TILE
    src_count = lax.axis_size("src")
    me_src = lax.axis_index("src")
    tiles = traces.reshape(comp_count, freq_count, TILE, per_rcv, TILE)
    assert comp_count == half_count
    half_tile = TILE // half_count
    arrived = []
    for step in range(per_rcv):
        pick = (me_src % per_rcv + step) % per_rcv
        sent = lax.dynamic_index_in_dim(tiles, pick, 3, keepdims=False)
        sent = lax.dynamic_slice_in_dim(sent, my_half * half_tile, half_tile, axis=3)
        got = lax.ppermute(sent, ("src", "rcv"), mirror_pairs(src_count, rcv_count, per_rcv, step))
        arrived.append(jnp.swapaxes(got, 2, 3))
    arrived = jnp.stack(arrived, axis=3)
    order = (me_src % per_rcv - jnp.arange(per_rcv)) % per_rcv
    rows_mine = jnp.take(arrived, order, axis=3)
    marks = (missing[0] > 0)[None, None, None, :, None]
    own_rows = lax.dynamic_slice_in_dim(tiles, my_half * half_tile, half_tile, axis=2)
    right_half = jnp.where(marks, rows_mine, own_rows).reshape(comp_count, freq_count, half_tile, local_cols)
    rows_other = lax.ppermute(rows_mine, "int", [(0, 1), (1, 0)])
    mirrored = jnp.stack([rows_mine, rows_other])
    mirrored = jnp.take(mirrored, (jnp.arange(half_count) + my_half) % half_count, axis=0)
    mirrored = jnp.moveaxis(mirrored, 0, 2).reshape(tiles.shape)
    filled = jnp.where(marks, mirrored, tiles).reshape(traces.shape)
    row_tiles = local_rows // TILE
    col_tiles = local_cols // TILE
    left_half = filled.reshape(comp_count, freq_count, local_rows, col_tiles, half_count, half_tile)
    left_half = lax.dynamic_index_in_dim(left_half, my_half, 4, keepdims=False)
    left_half = left_half.reshape(comp_count, freq_count, local_rows, col_tiles * half_tile)
    gathered = collect(left_half, "rcv", 3)
    block_count = gathered.shape[3] // half_tile
    chosen = (
        (aperture[:, :, None] == jnp.arange(block_count, dtype=jnp.int32)[None, None, :])
        .astype(jnp.float32)
        .sum(axis=1)
    )
    weighted = gathered.reshape(comp_count, freq_count, row_tiles, TILE, block_count, half_tile)
    weighted = (weighted * chosen[None, None, :, None, :, None]).reshape(
        comp_count, freq_count, local_rows, block_count * half_tile
    )
    slab_piece = lax.all_gather(right_half, "src", axis=2, tiled=True)
    out_cols = local_cols // half_count
    assert half_count == 2

    def half_product(which):
        cols = lax.dynamic_slice_in_dim(slab_piece, which * out_cols, out_cols, axis=3)
        real_part = complex_prod(weighted[0], cols[0]) - complex_prod(weighted[1], cols[1])
        imag_part = complex_prod(weighted[0], cols[1]) + complex_prod(weighted[1], cols[0])
        return jnp.stack([real_part, imag_part])

    sent = half_product(1 - my_half)
    got = lax.ppermute(sent, "int", [(0, 1), (1, 0)])
    my_share = half_product(my_half) + got
    kept_data = filled.reshape(comp_count, freq_count, local_rows, half_count, out_cols)
    kept_data = lax.dynamic_index_in_dim(kept_data, my_half, 3, keepdims=False)
    w_real = wavelet[0][:, None, None]
    w_imag = wavelet[1][:, None, None]
    out_real = kept_data[0] - (w_real * my_share[0] - w_imag * my_share[1])
    out_imag = kept_data[1] - (w_real * my_share[1] + w_imag * my_share[0])
    return jnp.stack([out_real, out_imag])


def solution(mesh):
    placed = (P(None, None, "src", "rcv"), P("src", "rcv"), P("src", None), P())
    return jax.shard_map(
        per_device,
        mesh=mesh,
        in_specs=placed,
        out_specs=P(None, None, "src", ("rcv", "int")),
        check_vma=False,
    )
```

```python
import jax
import jax.numpy as jnp
from jax import lax
from jax.sharding import PartitionSpec as P

TILE = 128


def from_everyone(x, axis):
    copies = jnp.broadcast_to(x, (lax.axis_size(axis), *x.shape))
    return lax.all_to_all(copies, axis, split_axis=0, concat_axis=0, tiled=True)


def joined_along(pieces, dim):
    pieces = jnp.moveaxis(pieces, 0, dim)
    lengths = pieces.shape
    return pieces.reshape(*lengths[:dim], lengths[dim] * lengths[dim + 1], *lengths[dim + 2 :])


def collect(x, axis, dim):
    pieces = from_everyone(x, axis)
    return joined_along(pieces, dim)


def in_blocks(x, dim, count):
    before, after = (x.shape[:dim], x.shape[dim + 1 :])
    return jnp.moveaxis(x.reshape(*before, count, -1, *after), dim, 0)


def sent_and_summed(x, axis, dim):
    pieces = in_blocks(x, dim, lax.axis_size(axis))
    arrived = lax.all_to_all(pieces, axis, split_axis=0, concat_axis=0, tiled=True)
    return arrived.sum(axis=0)


def mirror_pairs(n_src, n_rcv, per_rcv, step):
    pairs = []
    for s in range(n_src):
        for r in range(n_rcv):
            t = (s % per_rcv + step) % per_rcv
            dest_s = per_rcv * r + t
            if s > dest_s:
                pairs.append((s * n_rcv + r, dest_s * n_rcv + s // per_rcv))
    return pairs


def complex_prod(left_side, right_side):
    return jnp.einsum("fik,fkj->fij", left_side, right_side, precision=lax.Precision.HIGH)


def per_device(traces, missing, aperture, wavelet):
    half_count = lax.axis_size("int")
    my_half = lax.axis_index("int")
    rcv_count = lax.axis_size("rcv")
    comp_count, freq_count, local_rows, local_cols = traces.shape
    per_rcv = local_cols // TILE
    src_count = lax.axis_size("src")
    me_src = lax.axis_index("src")
    tiles = traces.reshape(comp_count, freq_count, TILE, per_rcv, TILE)
    assert comp_count == half_count
    half_tile = TILE // half_count
    arrived = []
    for step in range(per_rcv):
        pick = (me_src % per_rcv + step) % per_rcv
        sent = lax.dynamic_index_in_dim(tiles, pick, 3, keepdims=False)
        sent = lax.dynamic_slice_in_dim(sent, my_half * half_tile, half_tile, axis=3)
        got = lax.ppermute(sent, ("src", "rcv"), mirror_pairs(src_count, rcv_count, per_rcv, step))
        arrived.append(jnp.swapaxes(got, 2, 3))
    arrived = jnp.stack(arrived, axis=3)
    order = (me_src % per_rcv - jnp.arange(per_rcv)) % per_rcv
    rows_mine = jnp.take(arrived, order, axis=3)
    marks = (missing[0] > 0)[None, None, None, :, None]
    own_rows = lax.dynamic_slice_in_dim(tiles, my_half * half_tile, half_tile, axis=2)
    right_half = jnp.where(marks, rows_mine, own_rows).reshape(comp_count, freq_count, half_tile, local_cols)
    rows_other = lax.ppermute(rows_mine, "int", [(0, 1), (1, 0)])
    mirrored = jnp.stack([rows_mine, rows_other])
    mirrored = jnp.take(mirrored, (jnp.arange(half_count) + my_half) % half_count, axis=0)
    mirrored = jnp.moveaxis(mirrored, 0, 2).reshape(tiles.shape)
    filled = jnp.where(marks, mirrored, tiles).reshape(traces.shape)
    row_tiles = local_rows // TILE
    col_tiles = local_cols // TILE
    left_half = filled.reshape(comp_count, freq_count, local_rows, col_tiles, half_count, half_tile)
    left_half = lax.dynamic_index_in_dim(left_half, my_half, 4, keepdims=False)
    left_half = left_half.reshape(comp_count, freq_count, local_rows, col_tiles * half_tile)
    gathered = collect(left_half, "rcv", 3)
    block_count = gathered.shape[3] // half_tile
    chosen = (
        (aperture[:, :, None] == jnp.arange(block_count, dtype=jnp.int32)[None, None, :])
        .astype(jnp.float32)
        .sum(axis=1)
    )
    weighted = gathered.reshape(comp_count, freq_count, row_tiles, TILE, block_count, half_tile)
    weighted = (weighted * chosen[None, None, :, None, :, None]).reshape(
        comp_count, freq_count, local_rows, block_count * half_tile
    )
    slab_piece = lax.all_gather(right_half, "src", axis=2, tiled=True)
    out_cols = local_cols // half_count
    assert half_count == 2

    def half_product(which):
        cols = lax.dynamic_slice_in_dim(slab_piece, which * out_cols, out_cols, axis=3)
        real_part = complex_prod(weighted[0], cols[0]) - complex_prod(weighted[1], cols[1])
        imag_part = complex_prod(weighted[0], cols[1]) + complex_prod(weighted[1], cols[0])
        return jnp.stack([real_part, imag_part])

    sent = half_product(1 - my_half)
    sent, slab_piece = lax.optimization_barrier((sent, slab_piece))
    got = lax.ppermute(sent, "int", [(0, 1), (1, 0)])
    my_share = half_product(my_half) + got
    kept_data = filled.reshape(comp_count, freq_count, local_rows, half_count, out_cols)
    kept_data = lax.dynamic_index_in_dim(kept_data, my_half, 3, keepdims=False)
    w_real = wavelet[0][:, None, None]
    w_imag = wavelet[1][:, None, None]
    out_real = kept_data[0] - (w_real * my_share[0] - w_imag * my_share[1])
    out_imag = kept_data[1] - (w_real * my_share[1] + w_imag * my_share[0])
    return jnp.stack([out_real, out_imag])


def solution(mesh):
    placed = (P(None, None, "src", "rcv"), P("src", "rcv"), P("src", None), P())
    return jax.shard_map(
        per_device,
        mesh=mesh,
        in_specs=placed,
        out_specs=P(None, None, "src", ("rcv", "int")),
        check_vma=False,
    )
```

```python
import jax
import jax.numpy as jnp
from jax import lax
from jax.sharding import PartitionSpec as P

TILE = 128


def from_everyone(x, axis):
    copies = jnp.broadcast_to(x, (lax.axis_size(axis), *x.shape))
    return lax.all_to_all(copies, axis, split_axis=0, concat_axis=0, tiled=True)


def joined_along(pieces, dim):
    pieces = jnp.moveaxis(pieces, 0, dim)
    lengths = pieces.shape
    return pieces.reshape(*lengths[:dim], lengths[dim] * lengths[dim + 1], *lengths[dim + 2 :])


def collect(x, axis, dim):
    pieces = from_everyone(x, axis)
    return joined_along(pieces, dim)


def in_blocks(x, dim, count):
    before, after = (x.shape[:dim], x.shape[dim + 1 :])
    return jnp.moveaxis(x.reshape(*before, count, -1, *after), dim, 0)


def sent_and_summed(x, axis, dim):
    pieces = in_blocks(x, dim, lax.axis_size(axis))
    arrived = lax.all_to_all(pieces, axis, split_axis=0, concat_axis=0, tiled=True)
    return arrived.sum(axis=0)


def mirror_pairs(n_src, n_rcv, per_rcv, step):
    pairs = []
    for s in range(n_src):
        for r in range(n_rcv):
            t = (s % per_rcv + step) % per_rcv
            dest_s = per_rcv * r + t
            if s > dest_s:
                pairs.append((s * n_rcv + r, dest_s * n_rcv + s // per_rcv))
    return pairs


def complex_prod(left_side, right_side):
    return jnp.einsum("fik,fkj->fij", left_side, right_side, precision=lax.Precision.HIGH)


def per_device(traces, missing, aperture, wavelet):
    half_count = lax.axis_size("int")
    my_half = lax.axis_index("int")
    rcv_count = lax.axis_size("rcv")
    comp_count, freq_count, local_rows, local_cols = traces.shape
    per_rcv = local_cols // TILE
    src_count = lax.axis_size("src")
    me_src = lax.axis_index("src")
    tiles = traces.reshape(comp_count, freq_count, TILE, per_rcv, TILE)
    assert comp_count == half_count
    half_tile = TILE // half_count
    arrived = []
    for step in range(per_rcv):
        pick = (me_src % per_rcv + step) % per_rcv
        sent = lax.dynamic_index_in_dim(tiles, pick, 3, keepdims=False)
        sent = lax.dynamic_slice_in_dim(sent, my_half * half_tile, half_tile, axis=3)
        got = lax.ppermute(sent, ("src", "rcv"), mirror_pairs(src_count, rcv_count, per_rcv, step))
        arrived.append(jnp.swapaxes(got, 2, 3))
    arrived = jnp.stack(arrived, axis=3)
    order = (me_src % per_rcv - jnp.arange(per_rcv)) % per_rcv
    rows_mine = jnp.take(arrived, order, axis=3)
    marks = (missing[0] > 0)[None, None, None, :, None]
    own_rows = lax.dynamic_slice_in_dim(tiles, my_half * half_tile, half_tile, axis=2)
    right_half = jnp.where(marks, rows_mine, own_rows).reshape(comp_count, freq_count, half_tile, local_cols)
    rows_other = lax.ppermute(rows_mine, "int", [(0, 1), (1, 0)])
    mirrored = jnp.stack([rows_mine, rows_other])
    mirrored = jnp.take(mirrored, (jnp.arange(half_count) + my_half) % half_count, axis=0)
    mirrored = jnp.moveaxis(mirrored, 0, 2).reshape(tiles.shape)
    filled = jnp.where(marks, mirrored, tiles).reshape(traces.shape)
    row_tiles = local_rows // TILE
    col_tiles = local_cols // TILE
    left_half = filled.reshape(comp_count, freq_count, local_rows, col_tiles, half_count, half_tile)
    left_half = lax.dynamic_index_in_dim(left_half, my_half, 4, keepdims=False)
    left_half = left_half.reshape(comp_count, freq_count, local_rows, col_tiles * half_tile)
    gathered = collect(left_half, "rcv", 3)
    block_count = gathered.shape[3] // half_tile
    chosen = (
        (aperture[:, :, None] == jnp.arange(block_count, dtype=jnp.int32)[None, None, :])
        .astype(jnp.float32)
        .sum(axis=1)
    )
    weighted = gathered.reshape(comp_count, freq_count, row_tiles, TILE, block_count, half_tile)
    weighted = (weighted * chosen[None, None, :, None, :, None]).reshape(
        comp_count, freq_count, local_rows, block_count * half_tile
    )
    slab_piece = lax.all_gather(right_half, "src", axis=2, tiled=True)
    out_cols = local_cols // half_count
    assert half_count == 2

    def half_product(which):
        cols = slab_piece[..., which * out_cols : (which + 1) * out_cols]
        real_part = complex_prod(weighted[0], cols[0]) - complex_prod(weighted[1], cols[1])
        imag_part = complex_prod(weighted[0], cols[1]) + complex_prod(weighted[1], cols[0])
        return jnp.stack([real_part, imag_part])

    def chosen_half(first):
        return lax.cond(
            (my_half == 0) == first, lambda: half_product(1), lambda: half_product(0)
        )

    sent = chosen_half(True)
    got = lax.ppermute(sent, "int", [(0, 1), (1, 0)])
    my_share = chosen_half(False) + got
    kept_data = filled.reshape(comp_count, freq_count, local_rows, half_count, out_cols)
    kept_data = lax.dynamic_index_in_dim(kept_data, my_half, 3, keepdims=False)
    w_real = wavelet[0][:, None, None]
    w_imag = wavelet[1][:, None, None]
    out_real = kept_data[0] - (w_real * my_share[0] - w_imag * my_share[1])
    out_imag = kept_data[1] - (w_real * my_share[1] + w_imag * my_share[0])
    return jnp.stack([out_real, out_imag])


def solution(mesh):
    placed = (P(None, None, "src", "rcv"), P("src", "rcv"), P("src", None), P())
    return jax.shard_map(
        per_device,
        mesh=mesh,
        in_specs=placed,
        out_specs=P(None, None, "src", ("rcv", "int")),
        check_vma=False,
    )
```

```python
import jax
import jax.numpy as jnp
from jax import lax
from jax.sharding import PartitionSpec as P

TILE = 128


def from_everyone(x, axis):
    copies = jnp.broadcast_to(x, (lax.axis_size(axis), *x.shape))
    return lax.all_to_all(copies, axis, split_axis=0, concat_axis=0, tiled=True)


def joined_along(pieces, dim):
    pieces = jnp.moveaxis(pieces, 0, dim)
    lengths = pieces.shape
    return pieces.reshape(*lengths[:dim], lengths[dim] * lengths[dim + 1], *lengths[dim + 2 :])


def collect(x, axis, dim):
    pieces = from_everyone(x, axis)
    return joined_along(pieces, dim)


def in_blocks(x, dim, count):
    before, after = (x.shape[:dim], x.shape[dim + 1 :])
    return jnp.moveaxis(x.reshape(*before, count, -1, *after), dim, 0)


def sent_and_summed(x, axis, dim):
    pieces = in_blocks(x, dim, lax.axis_size(axis))
    arrived = lax.all_to_all(pieces, axis, split_axis=0, concat_axis=0, tiled=True)
    return arrived.sum(axis=0)


def mirror_pairs(n_src, n_rcv, per_rcv, step):
    pairs = []
    for s in range(n_src):
        for r in range(n_rcv):
            t = (s % per_rcv + step) % per_rcv
            dest_s = per_rcv * r + t
            if s > dest_s:
                pairs.append((s * n_rcv + r, dest_s * n_rcv + s // per_rcv))
    return pairs


def complex_prod(left_side, right_side):
    return jnp.einsum("fik,fkj->fij", left_side, right_side, precision=lax.Precision.HIGH)


def per_device(traces, missing, aperture, wavelet):
    half_count = lax.axis_size("int")
    my_half = lax.axis_index("int")
    rcv_count = lax.axis_size("rcv")
    comp_count, freq_count, local_rows, local_cols = traces.shape
    per_rcv = local_cols // TILE
    src_count = lax.axis_size("src")
    me_src = lax.axis_index("src")
    tiles = traces.reshape(comp_count, freq_count, TILE, per_rcv, TILE)
    assert comp_count == half_count
    half_tile = TILE // half_count
    arrived = []
    for step in range(per_rcv):
        pick = (me_src % per_rcv + step) % per_rcv
        sent = lax.dynamic_index_in_dim(tiles, pick, 3, keepdims=False)
        sent = lax.dynamic_slice_in_dim(sent, my_half * half_tile, half_tile, axis=3)
        got = lax.ppermute(sent, ("src", "rcv"), mirror_pairs(src_count, rcv_count, per_rcv, step))
        arrived.append(jnp.swapaxes(got, 2, 3))
    arrived = jnp.stack(arrived, axis=3)
    order = (me_src % per_rcv - jnp.arange(per_rcv)) % per_rcv
    rows_mine = jnp.take(arrived, order, axis=3)
    marks = (missing[0] > 0)[None, None, None, :, None]
    own_rows = lax.dynamic_slice_in_dim(tiles, my_half * half_tile, half_tile, axis=2)
    right_half = jnp.where(marks, rows_mine, own_rows).reshape(comp_count, freq_count, half_tile, local_cols)
    rows_other = lax.ppermute(rows_mine, "int", [(0, 1), (1, 0)])
    mirrored = jnp.stack([rows_mine, rows_other])
    mirrored = jnp.take(mirrored, (jnp.arange(half_count) + my_half) % half_count, axis=0)
    mirrored = jnp.moveaxis(mirrored, 0, 2).reshape(tiles.shape)
    filled = jnp.where(marks, mirrored, tiles).reshape(traces.shape)
    row_tiles = local_rows // TILE
    col_tiles = local_cols // TILE
    left_half = filled.reshape(comp_count, freq_count, local_rows, col_tiles, half_count, half_tile)
    left_half = lax.dynamic_index_in_dim(left_half, my_half, 4, keepdims=False)
    left_half = left_half.reshape(comp_count, freq_count, local_rows, col_tiles * half_tile)
    gathered = collect(left_half, "rcv", 3)
    block_count = gathered.shape[3] // half_tile
    chosen = (
        (aperture[:, :, None] == jnp.arange(block_count, dtype=jnp.int32)[None, None, :])
        .astype(jnp.float32)
        .sum(axis=1)
    )
    weighted = gathered.reshape(comp_count, freq_count, row_tiles, TILE, block_count, half_tile)
    weighted = (weighted * chosen[None, None, :, None, :, None]).reshape(
        comp_count, freq_count, local_rows, block_count * half_tile
    )
    slab_piece = lax.all_gather(right_half, "src", axis=2, tiled=True)
    out_cols = local_cols // half_count
    assert half_count == 2

    real_part = complex_prod(weighted[0], slab_piece[0]) - complex_prod(weighted[1], slab_piece[1])
    imag_part = complex_prod(weighted[0], slab_piece[1]) + complex_prod(weighted[1], slab_piece[0])
    partial_sum = jnp.stack([real_part, imag_part])
    sent = lax.dynamic_slice_in_dim(partial_sum, (1 - my_half) * out_cols, out_cols, axis=3)
    got = lax.ppermute(sent, "int", [(0, 1), (1, 0)])
    my_share = lax.dynamic_slice_in_dim(partial_sum, my_half * out_cols, out_cols, axis=3) + got
    kept_data = filled.reshape(comp_count, freq_count, local_rows, half_count, out_cols)
    kept_data = lax.dynamic_index_in_dim(kept_data, my_half, 3, keepdims=False)
    w_real = wavelet[0][:, None, None]
    w_imag = wavelet[1][:, None, None]
    out_real = kept_data[0] - (w_real * my_share[0] - w_imag * my_share[1])
    out_imag = kept_data[1] - (w_real * my_share[1] + w_imag * my_share[0])
    return jnp.stack([out_real, out_imag])


def solution(mesh):
    placed = (P(None, None, "src", "rcv"), P("src", "rcv"), P("src", None), P())
    return jax.shard_map(
        per_device,
        mesh=mesh,
        in_specs=placed,
        out_specs=P(None, None, "src", ("rcv", "int")),
        check_vma=False,
    )
```

```python
import jax
import jax.numpy as jnp
from jax import lax
from jax.sharding import PartitionSpec as P

TILE = 128


def from_everyone(x, axis):
    copies = jnp.broadcast_to(x, (lax.axis_size(axis), *x.shape))
    return lax.all_to_all(copies, axis, split_axis=0, concat_axis=0, tiled=True)


def joined_along(pieces, dim):
    pieces = jnp.moveaxis(pieces, 0, dim)
    lengths = pieces.shape
    return pieces.reshape(*lengths[:dim], lengths[dim] * lengths[dim + 1], *lengths[dim + 2 :])


def collect(x, axis, dim):
    pieces = from_everyone(x, axis)
    return joined_along(pieces, dim)


def in_blocks(x, dim, count):
    before, after = (x.shape[:dim], x.shape[dim + 1 :])
    return jnp.moveaxis(x.reshape(*before, count, -1, *after), dim, 0)


def sent_and_summed(x, axis, dim):
    pieces = in_blocks(x, dim, lax.axis_size(axis))
    arrived = lax.all_to_all(pieces, axis, split_axis=0, concat_axis=0, tiled=True)
    return arrived.sum(axis=0)


def mirror_pairs(n_src, n_rcv, per_rcv, step):
    pairs = []
    for s in range(n_src):
        for r in range(n_rcv):
            t = (s % per_rcv + step) % per_rcv
            dest_s = per_rcv * r + t
            if s > dest_s:
                pairs.append((s * n_rcv + r, dest_s * n_rcv + s // per_rcv))
    return pairs


def complex_prod(left_side, right_side):
    return jnp.einsum("fik,fkj->fij", left_side, right_side, precision=lax.Precision.HIGH)


def per_device(traces, missing, aperture, wavelet):
    half_count = lax.axis_size("int")
    my_half = lax.axis_index("int")
    rcv_count = lax.axis_size("rcv")
    comp_count, freq_count, local_rows, local_cols = traces.shape
    per_rcv = local_cols // TILE
    src_count = lax.axis_size("src")
    me_src = lax.axis_index("src")
    tiles = traces.reshape(comp_count, freq_count, TILE, per_rcv, TILE)
    assert comp_count == half_count
    half_tile = TILE // half_count
    arrived = []
    for step in range(per_rcv):
        pick = (me_src % per_rcv + step) % per_rcv
        sent = lax.dynamic_index_in_dim(tiles, pick, 3, keepdims=False)
        sent = lax.dynamic_slice_in_dim(sent, my_half * half_tile, half_tile, axis=3)
        got = lax.ppermute(sent, ("src", "rcv"), mirror_pairs(src_count, rcv_count, per_rcv, step))
        arrived.append(jnp.swapaxes(got, 2, 3))
    arrived = jnp.stack(arrived, axis=3)
    order = (me_src % per_rcv - jnp.arange(per_rcv)) % per_rcv
    rows_mine = jnp.take(arrived, order, axis=3)
    marks = (missing[0] > 0)[None, None, None, :, None]
    own_rows = lax.dynamic_slice_in_dim(tiles, my_half * half_tile, half_tile, axis=2)
    right_half = jnp.where(marks, rows_mine, own_rows).reshape(comp_count, freq_count, half_tile, local_cols)
    rows_other = lax.ppermute(rows_mine, "int", [(0, 1), (1, 0)])
    mirrored = jnp.stack([rows_mine, rows_other])
    mirrored = jnp.take(mirrored, (jnp.arange(half_count) + my_half) % half_count, axis=0)
    mirrored = jnp.moveaxis(mirrored, 0, 2).reshape(tiles.shape)
    filled = jnp.where(marks, mirrored, tiles).reshape(traces.shape)
    row_tiles = local_rows // TILE
    col_tiles = local_cols // TILE
    left_half = filled.reshape(comp_count, freq_count, local_rows, col_tiles, half_count, half_tile)
    left_half = lax.dynamic_index_in_dim(left_half, my_half, 4, keepdims=False)
    left_half = left_half.reshape(comp_count, freq_count, local_rows, col_tiles * half_tile)
    gathered = collect(left_half, "rcv", 3)
    block_count = gathered.shape[3] // half_tile
    chosen = (
        (aperture[:, :, None] == jnp.arange(block_count, dtype=jnp.int32)[None, None, :])
        .astype(jnp.float32)
        .sum(axis=1)
    )
    weighted = gathered.reshape(comp_count, freq_count, row_tiles, TILE, block_count, half_tile)
    weighted = (weighted * chosen[None, None, :, None, :, None]).reshape(
        comp_count, freq_count, local_rows, block_count * half_tile
    )
    slab_piece = right_half.reshape(comp_count * freq_count, half_tile, local_cols)
    slab_piece = lax.all_gather(slab_piece, "src", axis=1, tiled=True)
    slab_piece = slab_piece.reshape(comp_count, freq_count, -1, local_cols)
    out_cols = local_cols // half_count
    assert half_count == 2

    real_part = complex_prod(weighted[0], slab_piece[0]) - complex_prod(weighted[1], slab_piece[1])
    imag_part = complex_prod(weighted[0], slab_piece[1]) + complex_prod(weighted[1], slab_piece[0])
    partial_sum = jnp.stack([real_part, imag_part])
    sent = lax.dynamic_slice_in_dim(partial_sum, (1 - my_half) * out_cols, out_cols, axis=3)
    got = lax.ppermute(sent, "int", [(0, 1), (1, 0)])
    my_share = lax.dynamic_slice_in_dim(partial_sum, my_half * out_cols, out_cols, axis=3) + got
    kept_data = filled.reshape(comp_count, freq_count, local_rows, half_count, out_cols)
    kept_data = lax.dynamic_index_in_dim(kept_data, my_half, 3, keepdims=False)
    w_real = wavelet[0][:, None, None]
    w_imag = wavelet[1][:, None, None]
    out_real = kept_data[0] - (w_real * my_share[0] - w_imag * my_share[1])
    out_imag = kept_data[1] - (w_real * my_share[1] + w_imag * my_share[0])
    return jnp.stack([out_real, out_imag])


def solution(mesh):
    placed = (P(None, None, "src", "rcv"), P("src", "rcv"), P("src", None), P())
    return jax.shard_map(
        per_device,
        mesh=mesh,
        in_specs=placed,
        out_specs=P(None, None, "src", ("rcv", "int")),
        check_vma=False,
    )
```

```python
import jax
import jax.numpy as jnp
from jax import lax
from jax.sharding import PartitionSpec as P

TILE = 128


def from_everyone(x, axis):
    copies = jnp.broadcast_to(x, (lax.axis_size(axis), *x.shape))
    return lax.all_to_all(copies, axis, split_axis=0, concat_axis=0, tiled=True)


def joined_along(pieces, dim):
    pieces = jnp.moveaxis(pieces, 0, dim)
    lengths = pieces.shape
    return pieces.reshape(*lengths[:dim], lengths[dim] * lengths[dim + 1], *lengths[dim + 2 :])


def collect(x, axis, dim):
    pieces = from_everyone(x, axis)
    return joined_along(pieces, dim)


def in_blocks(x, dim, count):
    before, after = (x.shape[:dim], x.shape[dim + 1 :])
    return jnp.moveaxis(x.reshape(*before, count, -1, *after), dim, 0)


def sent_and_summed(x, axis, dim):
    pieces = in_blocks(x, dim, lax.axis_size(axis))
    arrived = lax.all_to_all(pieces, axis, split_axis=0, concat_axis=0, tiled=True)
    return arrived.sum(axis=0)


def mirror_pairs(n_src, n_rcv, per_rcv, step):
    pairs = []
    for s in range(n_src):
        for r in range(n_rcv):
            t = (s % per_rcv + step) % per_rcv
            dest_s = per_rcv * r + t
            if s > dest_s:
                pairs.append((s * n_rcv + r, dest_s * n_rcv + s // per_rcv))
    return pairs


def complex_prod(left_side, right_side):
    return jnp.einsum("fik,fkj->fij", left_side, right_side, precision=lax.Precision.HIGH)


def per_device(traces, missing, aperture, wavelet):
    half_count = lax.axis_size("int")
    my_half = lax.axis_index("int")
    rcv_count = lax.axis_size("rcv")
    comp_count, freq_count, local_rows, local_cols = traces.shape
    per_rcv = local_cols // TILE
    src_count = lax.axis_size("src")
    me_src = lax.axis_index("src")
    tiles = traces.reshape(comp_count, freq_count, TILE, per_rcv, TILE)
    assert comp_count == half_count
    half_tile = TILE // half_count
    arrived = []
    for step in range(per_rcv):
        pick = (me_src % per_rcv + step) % per_rcv
        sent = lax.dynamic_index_in_dim(tiles, pick, 3, keepdims=False)
        sent = lax.dynamic_slice_in_dim(sent, my_half * half_tile, half_tile, axis=3)
        got = lax.ppermute(sent, ("src", "rcv"), mirror_pairs(src_count, rcv_count, per_rcv, step))
        arrived.append(jnp.swapaxes(got, 2, 3))
    arrived = jnp.stack(arrived, axis=3)
    order = (me_src % per_rcv - jnp.arange(per_rcv)) % per_rcv
    rows_mine = jnp.take(arrived, order, axis=3)
    marks = (missing[0] > 0)[None, None, None, :, None]
    own_rows = lax.dynamic_slice_in_dim(tiles, my_half * half_tile, half_tile, axis=2)
    right_half = jnp.where(marks, rows_mine, own_rows).reshape(comp_count, freq_count, half_tile, local_cols)
    rows_other = lax.ppermute(rows_mine, "int", [(0, 1), (1, 0)])
    mirrored = jnp.stack([rows_mine, rows_other])
    mirrored = jnp.take(mirrored, (jnp.arange(half_count) + my_half) % half_count, axis=0)
    mirrored = jnp.moveaxis(mirrored, 0, 2).reshape(tiles.shape)
    filled = jnp.where(marks, mirrored, tiles).reshape(traces.shape)
    row_tiles = local_rows // TILE
    col_tiles = local_cols // TILE
    left_half = filled.reshape(comp_count, freq_count, local_rows, col_tiles, half_count, half_tile)
    left_half = lax.dynamic_index_in_dim(left_half, my_half, 4, keepdims=False)
    left_half = left_half.reshape(comp_count, freq_count, local_rows, col_tiles * half_tile)
    gathered = collect(left_half, "rcv", 3)
    block_count = gathered.shape[3] // half_tile
    chosen = (
        (aperture[:, :, None] == jnp.arange(block_count, dtype=jnp.int32)[None, None, :])
        .astype(jnp.float32)
        .sum(axis=1)
    )
    weighted = gathered.reshape(comp_count, freq_count, row_tiles, TILE, block_count, half_tile)
    weighted = (weighted * chosen[None, None, :, None, :, None]).reshape(
        comp_count, freq_count, local_rows, block_count * half_tile
    )
    slab_piece = right_half.reshape(comp_count * freq_count, half_tile, local_cols)
    slab_piece = lax.all_gather(slab_piece, "src", axis=1, tiled=True)
    slab_piece = slab_piece.reshape(comp_count, freq_count, -1, local_cols)
    out_cols = local_cols // half_count
    assert half_count == 2

    def half_product(which):
        cols = lax.dynamic_slice_in_dim(slab_piece, which * out_cols, out_cols, axis=3)
        real_part = complex_prod(weighted[0], cols[0]) - complex_prod(weighted[1], cols[1])
        imag_part = complex_prod(weighted[0], cols[1]) + complex_prod(weighted[1], cols[0])
        return jnp.stack([real_part, imag_part])

    sent = half_product(1 - my_half)
    got = lax.ppermute(sent, "int", [(0, 1), (1, 0)])
    my_share = half_product(my_half) + got
    kept_data = filled.reshape(comp_count, freq_count, local_rows, half_count, out_cols)
    kept_data = lax.dynamic_index_in_dim(kept_data, my_half, 3, keepdims=False)
    w_real = wavelet[0][:, None, None]
    w_imag = wavelet[1][:, None, None]
    out_real = kept_data[0] - (w_real * my_share[0] - w_imag * my_share[1])
    out_imag = kept_data[1] - (w_real * my_share[1] + w_imag * my_share[0])
    return jnp.stack([out_real, out_imag])


def solution(mesh):
    placed = (P(None, None, "src", "rcv"), P("src", "rcv"), P("src", None), P())
    return jax.shard_map(
        per_device,
        mesh=mesh,
        in_specs=placed,
        out_specs=P(None, None, "src", ("rcv", "int")),
        check_vma=False,
    )
```
